512 devices in a mesh: dp: 8 (over y), expert: 64 (over x, z, core).
Axes of the slice: x: 4, y: 8, z: 8, core: 2. Of those that a mesh axis runs over, the one named last changes fastest.
Arguments:
- tokens: bfloat16 [65536, 3584], P(('dp', 'expert')), may hold values from -6 to 6
- out_cotangent: bfloat16 [65536, 3584], P(('dp', 'expert')), may hold values from -6 to 6
- expert_ids: int32 [65536, 8], P(('dp', 'expert')), may hold values from 0 to 255, as said below
- gate_fixed: int32 [65536, 8], P(('dp', 'expert')), may hold values from 4096 to 65535
- w_gate: bfloat16 [64, 3584, 128], P('expert', 'dp'), may hold values from -0.09375 to 0.09375
- w_up: bfloat16 [64, 3584, 128], P('expert', 'dp'), may hold values from -0.09375 to 0.09375
- w_down: bfloat16 [64, 3584, 128], P('expert', 'dp'), may hold values from -0.125 to 0.125
Outputs:
- layer_out: bfloat16 [65536, 3584], P(('dp', 'expert'))
- token_grad: bfloat16 [65536, 3584], P(('dp', 'expert'))
- grad_gate: float32 [64, 3584, 128], P('expert', 'dp')
- grad_up: float32 [64, 3584, 128], P('expert', 'dp')
- grad_down: float32 [64, 3584, 128], P('expert', 'dp')
The draws below stay inside these ranges and needn't reach their ends.
Inputs may be any that keep to these rules, and one draw needn't show every extreme that they name: `expert_ids`: each row names 8 different experts. Within the 128 rows of one device each expert below 4 is named by 1 to 4 rows; in every draw one expert below 4 is named by exactly 4 rows on every device.
All inputs are finite; a program needn't handle non-finite values.
Results may differ from the reference program's by a relative error of at most 0.014.
Values may be sent and summed in bfloat16 or wider, within the bound.
No kernel may reach another device: no remote copies, remote signals or barrier semaphores. Data moves between devices by JAX's collectives and lax.ppermute only.
A program may use at most 128 MiB of HBM per device.

```python
import jax
import jax.numpy as jnp
from jax import lax

D = 3584
HIDDEN_SIZE = 2048
EXPERTS_ALL = 256
TOP = 8
SPLIT = 16
CAP = 4
TOK_DEV = 128
HID_DEV = 128
EXP_WIN = 4
SHARDS = 64
TOKENS = 65536
N_DP = 8


def draw_expert_ids(key, part):
    blocks = TOKENS // TOK_DEV
    others_count = EXPERTS_ALL - EXP_WIN
    keys = jax.random.split(jax.random.fold_in(key, 7), 5)
    counts = jax.random.randint(keys[0], (blocks, EXP_WIN), 1, CAP + 1)
    hot = jax.random.randint(keys[1], (), 0, EXP_WIN)
    column = jnp.arange(EXP_WIN, dtype=jnp.int32)
    counts = jnp.where(column[None, :] == hot, CAP, counts)
    scores = jax.random.randint(keys[2], (blocks, EXP_WIN, TOK_DEV), 0, 1 << 20) * TOK_DEV
    scores = scores + jnp.arange(TOK_DEV, dtype=jnp.int32)[None, None, :]
    ranks = jnp.argsort(jnp.argsort(scores, axis=-1), axis=-1)
    member = ranks < counts[:, :, None]
    member = jnp.transpose(member, (0, 2, 1)).reshape(TOKENS, EXP_WIN)
    other_scores = jax.random.randint(keys[3], (TOKENS, others_count), 0, 1 << 20) * 256
    other_scores = other_scores + jnp.arange(others_count, dtype=jnp.int32)[None, :]
    unused, others = lax.top_k(other_scores, TOP)
    others = others.astype(jnp.int32) + EXP_WIN
    running = jnp.cumsum(member.astype(jnp.int32), axis=1)
    total = running[:, -1:]
    slots = jnp.arange(TOP, dtype=jnp.int32)
    match = jnp.logical_and(member[:, :, None], running[:, :, None] == slots[None, None, :] + 1)
    win_id = jnp.sum(jnp.where(match, column[None, :, None], 0), axis=1)
    index = jnp.clip(slots[None, :] - total, 0, TOP - 1)
    other_id = jnp.take_along_axis(others, index, axis=1)
    chosen = jnp.where(slots[None, :] < total, win_id, other_id)
    order_scores = jax.random.randint(keys[4], (TOKENS, TOP), 0, 1 << 20) * TOP + slots[None, :]
    order = jnp.argsort(order_scores, axis=1)
    return jnp.take_along_axis(chosen, order, axis=1).astype(jnp.int32)


def set_ends(drawn, key, smallest, top_value):
    dims = drawn.shape
    index_at = [jax.random.randint(jax.random.fold_in(key, axis), (), 0, dims[axis]) for axis in range(len(dims))]
    drawn = drawn.at[tuple(index_at)].set(smallest)
    longest = dims.index(max(dims))
    index_at[longest] = (index_at[longest] + 1) % dims[longest]
    return drawn.at[tuple(index_at)].set(top_value)


def shard_levels(stream_key, dims, cuts, low, top_value):
    def one(axis_at, shards_of):
        steps = jax.random.uniform(jax.random.fold_in(jax.random.fold_in(stream_key, 6), axis_at), (shards_of,), jnp.float32, low / len(cuts), top_value / len(cuts))
        return jnp.repeat(jnp.exp(steps), dims[axis_at] // shards_of).reshape((-1,) + (1,) * (len(dims) - axis_at - 1))

    factor_of = one(*cuts[0])
    for cut in cuts[1:]:
        factor_of = factor_of * one(*cut)
    return factor_of


def scatter_about(rng, extent, width, most, cuts=(), kind=jnp.bfloat16):
    array = width * jax.random.normal(rng, extent, jnp.float32)
    if cuts:
        array = array * shard_levels(rng, extent, cuts, -0.22, 0.18)
    return jnp.clip(array, -most, most).astype(kind)


def setup_inputs(seed: int = 0) -> dict:
    key_list = jax.random.split(jax.random.key(seed), 8)
    tokens = scatter_about(key_list[0], (TOKENS, D), 1.0, 6.0, ((0, 512),))
    out_cotangent = scatter_about(key_list[1], (TOKENS, D), 1.0, 6.0, ((0, 512),))
    expert_ids = draw_expert_ids(jax.random.fold_in(key_list[7], 71), 0)
    gate_fixed = set_ends(jax.random.randint(key_list[3], (TOKENS, TOP), 4096, 65536), jax.random.fold_in(key_list[3], 1), 4096, 65535).astype(jnp.int32)
    w_gate = scatter_about(key_list[4], (SHARDS, D, HID_DEV), D ** -0.5, 0.09375, ((0, 64), (1, 8)))
    w_up = scatter_about(key_list[5], (SHARDS, D, HID_DEV), D ** -0.5, 0.09375, ((0, 64), (1, 8)))
    w_down = scatter_about(key_list[6], (SHARDS, D, HID_DEV), HIDDEN_SIZE ** -0.5, 0.125, ((0, 64), (1, 8)))
    return {"tokens": tokens, "out_cotangent": out_cotangent, "expert_ids": expert_ids, "gate_fixed": gate_fixed, "w_gate": w_gate, "w_up": w_up, "w_down": w_down}


SCALE = 2.0 ** -16
HIGH = lax.Precision.HIGHEST


def routing(ids, gates):
    wanted = jnp.arange(EXP_WIN, dtype=jnp.int32)
    hits = ids[:, :, None] == wanted[None, None, :]
    member = jnp.any(hits, axis=1)
    weight = jnp.sum(jnp.where(hits, gates[:, :, None], 0), axis=1).astype(jnp.float32) * SCALE
    rank = jnp.cumsum(member.astype(jnp.int32), axis=0) - 1
    slots = jnp.arange(CAP, dtype=jnp.int32)
    pick = jnp.logical_and(member[:, :, None], rank[:, :, None] == slots[None, None, :])
    select = jnp.where(pick, 1.0, 0.0).astype(jnp.float32)
    slot_gate = jnp.sum(select * weight[:, :, None], axis=0)
    return select, slot_gate


def expert_weights(shards):
    full = shards.reshape(EXP_WIN, SPLIT, D, HID_DEV).transpose(0, 2, 1, 3)
    return full.reshape(EXP_WIN, D, HIDDEN_SIZE)


def shard_layout(grads):
    return grads.reshape(EXP_WIN, D, SPLIT, HID_DEV).transpose(0, 2, 1, 3).reshape(EXP_WIN * SPLIT, D, HID_DEV)


def reference(tokens, out_cotangent, expert_ids, gate_fixed, w_gate, w_up, w_down):
    blocks = TOKENS // TOK_DEV
    tok3 = tokens.reshape(blocks, TOK_DEV, D).astype(jnp.float32)
    cot3 = out_cotangent.reshape(blocks, TOK_DEV, D).astype(jnp.float32)
    select, slot_gate = jax.vmap(routing)(expert_ids.reshape(blocks, TOK_DEV, TOP),
                                          gate_fixed.reshape(blocks, TOK_DEV, TOP))
    slot_tokens = jnp.einsum('btec,btd->ebcd', select, tok3, precision=HIGH).astype(jnp.bfloat16)
    picked = jnp.einsum('btec,btd->ebcd', select, cot3, precision=HIGH)
    slot_cot = (jnp.transpose(slot_gate, (1, 0, 2))[:, :, :, None] * picked).astype(jnp.bfloat16)
    wg_all = expert_weights(w_gate)
    wu_all = expert_weights(w_up)
    wd_all = expert_weights(w_down)

    def one_expert(items):
        xs, dos, wg, wu, wd = items
        rows = xs.reshape(blocks * CAP, D)
        drows = dos.reshape(blocks * CAP, D)
        gate_pre = jnp.dot(rows, wg, preferred_element_type=jnp.float32)
        up_pre = jnp.dot(rows, wu, preferred_element_type=jnp.float32)
        sig = jax.nn.sigmoid(gate_pre)
        act = gate_pre * sig
        hidden = (act * up_pre).astype(jnp.bfloat16)
        expert_out = jnp.dot(hidden, wd.T, preferred_element_type=jnp.float32).astype(jnp.bfloat16)
        d_hidden = jnp.dot(drows, wd, preferred_element_type=jnp.float32)
        d_gate = (d_hidden * up_pre * sig * (1.0 + gate_pre * (1.0 - sig))).astype(jnp.bfloat16)
        d_up = (d_hidden * act).astype(jnp.bfloat16)
        slot_grad = (jnp.dot(d_gate, wg.T, preferred_element_type=jnp.float32)
                     + jnp.dot(d_up, wu.T, preferred_element_type=jnp.float32)).astype(jnp.bfloat16)
        xpart = rows.reshape(N_DP, -1, D).astype(jnp.float32)
        dpart = drows.reshape(N_DP, -1, D).astype(jnp.float32)

        def partial_sum(left, right):
            terms = jnp.einsum('prd,prh->pdh', left, right.reshape(N_DP, -1, HIDDEN_SIZE).astype(jnp.float32), precision=HIGH)
            return jnp.sum(terms.astype(jnp.bfloat16).astype(jnp.float32), axis=0)

        grad_g = partial_sum(xpart, d_gate)
        grad_u = partial_sum(xpart, d_up)
        grad_d = partial_sum(dpart, hidden)
        return (expert_out.reshape(blocks, CAP, D), slot_grad.reshape(blocks, CAP, D), grad_g, grad_u, grad_d)

    outs, grads, grad_g, grad_u, grad_d = lax.map(one_expert, (slot_tokens, slot_cot, wg_all, wu_all, wd_all))
    weighted = select * slot_gate[:, None, :, :]
    layer_out = jnp.einsum('btec,ebcd->btd', weighted, outs.astype(jnp.float32), precision=HIGH)
    token_grad = jnp.einsum('btec,ebcd->btd', select, grads.astype(jnp.float32), precision=HIGH)
    return (layer_out.astype(jnp.bfloat16).reshape(TOKENS, D),
            token_grad.astype(jnp.bfloat16).reshape(TOKENS, D),
            shard_layout(grad_g), shard_layout(grad_u), shard_layout(grad_d))
```

```python
import jax
import jax.numpy as jnp
from jax import lax
from jax.sharding import Mesh
from jax.sharding import PartitionSpec as P

SPLIT = 16
CAP = 4


SCALE = 2.0 ** (-16)
HIGH = lax.Precision.HIGHEST
TOK = ("dp", "ex", "eh")


def routing(ids, gates, window, capacity):
    wanted = jnp.arange(window, dtype=jnp.int32)
    hits = ids[:, :, None] == wanted[None, None, :]
    member = jnp.any(hits, axis=1)
    weight = jnp.sum(jnp.where(hits, gates[:, :, None], 0), axis=1).astype(jnp.float32) * SCALE
    rank = jnp.cumsum(member.astype(jnp.int32), axis=0) - 1
    slots = jnp.arange(capacity, dtype=jnp.int32)
    pick = jnp.logical_and(member[:, :, None], rank[:, :, None] == slots[None, None, :])
    select = jnp.where(pick, 1.0, 0.0).astype(jnp.float32)
    slot_gate = jnp.sum(select * weight[:, :, None], axis=0)
    return (select, slot_gate)


def expert_math(inputs, cotangents, w_all, hid):
    gate_w = w_all[:, :hid]
    up_w = w_all[:, hid : 2 * hid]
    down_w = w_all[:, 2 * hid :]
    f32 = jnp.float32
    gate_pre = jnp.dot(inputs, gate_w, preferred_element_type=f32)
    up_pre = jnp.dot(inputs, up_w, preferred_element_type=f32)
    sig = jax.nn.sigmoid(gate_pre)
    act = gate_pre * sig
    hidden = (act * up_pre).astype(jnp.bfloat16)
    partial_out = lax.dot_general(hidden, down_w, (((1,), (1,)), ((), ())), preferred_element_type=f32)
    d_hidden = jnp.dot(cotangents, down_w, preferred_element_type=f32)
    d_gate = (d_hidden * up_pre * sig * (1.0 + gate_pre * (1.0 - sig))).astype(jnp.bfloat16)
    d_up = (d_hidden * act).astype(jnp.bfloat16)
    partial_grad = lax.dot_general(
        d_gate, gate_w, (((1,), (1,)), ((), ())), preferred_element_type=f32
    ) + lax.dot_general(d_up, up_w, (((1,), (1,)), ((), ())), preferred_element_type=f32)
    tn = (((0,), (0,)), ((), ()))
    term = jnp.concatenate(
        [
            lax.dot_general(inputs, d_gate, tn, preferred_element_type=f32),
            lax.dot_general(inputs, d_up, tn, preferred_element_type=f32),
            lax.dot_general(cotangents, hidden, tn, preferred_element_type=f32),
        ],
        axis=1,
    )
    return (partial_out, partial_grad, term)


def per_device(tokens, out_cotangent, expert_ids, gate_fixed, w_gate, w_up, w_down):
    tok_rows, width = tokens.shape
    window = lax.axis_size("ex")
    hsplit = lax.axis_size("eh")
    hid = w_gate.shape[2]
    select, slot_gate = routing(expert_ids, gate_fixed, window, CAP)
    select_b = select.astype(jnp.bfloat16)
    slot_tokens = jnp.einsum(
        "tec,tf->ecf", select_b, tokens, preferred_element_type=jnp.float32
    ).astype(jnp.bfloat16)
    picked = jnp.einsum("tec,tf->ecf", select_b, out_cotangent, preferred_element_type=jnp.float32)
    slot_cot = (picked * slot_gate[:, :, None]).astype(jnp.bfloat16)
    payload = jnp.stack([slot_tokens, slot_cot], axis=1)
    w_loc = jnp.concatenate([w_gate[0], w_up[0], w_down[0]], axis=1)
    w_all = lax.all_gather(w_loc, "dp", axis=0, tiled=False)
    w_all = w_all.reshape(-1, 3 * hid)
    by_x = lax.all_to_all(payload, "ex", split_axis=0, concat_axis=0, tiled=True)
    arrived = lax.all_gather(by_x, "eh", axis=0, tiled=False)
    inputs = arrived[:, :, 0].reshape(hsplit * window * CAP, width)
    cotangents = arrived[:, :, 1].reshape(hsplit * window * CAP, width)
    partial_out, partial_grad, term = expert_math(inputs, cotangents, w_all, hid)
    summed = lax.psum_scatter(
        term.astype(jnp.bfloat16), "dp", scatter_dimension=0, tiled=True
    ).astype(jnp.float32)
    grad_gate = summed[:, :hid][None]
    grad_up = summed[:, hid : 2 * hid][None]
    grad_down = summed[:, 2 * hid :][None]
    results = jnp.stack(
        [
            partial_out.reshape(hsplit, window, CAP, width),
            partial_grad.reshape(hsplit, window, CAP, width),
        ],
        axis=2,
    ).astype(jnp.bfloat16)
    reduced = lax.psum_scatter(results, "eh", scatter_dimension=0, tiled=True)
    combined = lax.all_to_all(reduced[0], "ex", split_axis=0, concat_axis=0, tiled=True)
    combined = combined.astype(jnp.float32)
    weighted = select * slot_gate[None, :, :]
    layer_out = jnp.einsum("tec,ecf->tf", weighted, combined[:, 0], precision=HIGH)
    token_grad = jnp.einsum("tec,ecf->tf", select, combined[:, 1], precision=HIGH)
    return (
        layer_out.astype(jnp.bfloat16),
        token_grad.astype(jnp.bfloat16),
        grad_gate,
        grad_up,
        grad_down,
    )


def solution(mesh):
    n_dp = mesh.shape["dp"]
    n_exp = mesh.shape["expert"]
    devices = mesh.devices.reshape(n_dp, n_exp // SPLIT, SPLIT)
    grid = Mesh(devices, ("dp", "ex", "eh"))
    tok = P(TOK, None)
    wsp = P(("ex", "eh"), "dp", None)
    return jax.shard_map(
        per_device,
        mesh=grid,
        in_specs=(tok, tok, tok, tok, wsp, wsp, wsp),
        out_specs=(tok, tok, wsp, wsp, wsp),
        check_vma=False,
    )
```

```python
import jax
import jax.numpy as jnp
from jax import lax
from jax.sharding import PartitionSpec as P

SPLIT = 16
CAP = 4


SCALE = 2.0 ** (-16)
HIGH = lax.Precision.HIGHEST


def routing(ids, gates, window, capacity):
    wanted = jnp.arange(window, dtype=jnp.int32)
    hits = ids[:, :, None] == wanted[None, None, :]
    member = jnp.any(hits, axis=1)
    weight = jnp.sum(jnp.where(hits, gates[:, :, None], 0), axis=1).astype(jnp.float32) * SCALE
    rank = jnp.cumsum(member.astype(jnp.int32), axis=0) - 1
    slots = jnp.arange(capacity, dtype=jnp.int32)
    pick = jnp.logical_and(member[:, :, None], rank[:, :, None] == slots[None, None, :])
    select = jnp.where(pick, 1.0, 0.0).astype(jnp.float32)
    slot_gate = jnp.sum(select * weight[:, :, None], axis=0)
    return (select, slot_gate)


def expert_math(inputs, cotangents, gate_w, up_w, down_w):
    gate_pre = jnp.einsum("prf,pfh->rh", inputs, gate_w, preferred_element_type=jnp.float32)
    up_pre = jnp.einsum("prf,pfh->rh", inputs, up_w, preferred_element_type=jnp.float32)
    sig = jax.nn.sigmoid(gate_pre)
    act = gate_pre * sig
    hidden = (act * up_pre).astype(jnp.bfloat16)
    partial_out = jnp.einsum("rh,pfh->prf", hidden, down_w, preferred_element_type=jnp.float32)
    d_hidden = jnp.einsum("prf,pfh->rh", cotangents, down_w, preferred_element_type=jnp.float32)
    d_gate = (d_hidden * up_pre * sig * (1.0 + gate_pre * (1.0 - sig))).astype(jnp.bfloat16)
    d_up = (d_hidden * act).astype(jnp.bfloat16)
    partial_grad = jnp.einsum(
        "rh,pfh->prf", d_gate, gate_w, preferred_element_type=jnp.float32
    ) + jnp.einsum("rh,pfh->prf", d_up, up_w, preferred_element_type=jnp.float32)
    term = jnp.concatenate(
        [
            jnp.einsum("prf,rh->pfh", inputs, d_gate, preferred_element_type=jnp.float32),
            jnp.einsum("prf,rh->pfh", inputs, d_up, preferred_element_type=jnp.float32),
            jnp.einsum("prf,rh->pfh", cotangents, hidden, preferred_element_type=jnp.float32),
        ],
        axis=2,
    )
    return (partial_out, partial_grad, term.reshape(-1, term.shape[2]))


def per_device(tokens, out_cotangent, expert_ids, gate_fixed, w_gate, w_up, w_down):
    tok_rows, width = tokens.shape
    groups = lax.axis_size("expert")
    window = groups // SPLIT
    hid = w_gate.shape[2]
    parts = 1
    feat = width // parts
    select, slot_gate = routing(expert_ids, gate_fixed, window, CAP)
    select_b = select.astype(jnp.bfloat16)
    tok3 = tokens.reshape(tok_rows, parts, feat)
    cot3 = out_cotangent.reshape(tok_rows, parts, feat)
    slot_tokens = jnp.einsum(
        "tec,tsf->escf", select_b, tok3, preferred_element_type=jnp.float32
    ).astype(jnp.bfloat16)
    picked = jnp.einsum("tec,tsf->escf", select_b, cot3, preferred_element_type=jnp.float32)
    slot_cot = (picked * slot_gate[:, None, :, None]).astype(jnp.bfloat16)
    payload = jnp.stack([slot_tokens, slot_cot], axis=2)
    w_loc = jnp.concatenate([w_gate[0], w_up[0], w_down[0]], axis=1)
    w_all = lax.all_gather(w_loc, "dp", axis=0, tiled=False).reshape(-1, 3 * hid)
    gate_full = w_all[None, :, :hid]
    up_full = w_all[None, :, hid : 2 * hid]
    down_full = w_all[None, :, 2 * hid :]
    outgoing = jnp.broadcast_to(payload, (window, SPLIT, 2, CAP, width)).reshape(
        groups, 2, CAP, width
    )
    arrived = lax.all_to_all(outgoing, "expert", split_axis=0, concat_axis=0, tiled=True)
    pieces = arrived[None]
    inputs = pieces[:, :, 0].reshape(parts, groups * CAP, feat)
    cotangents = pieces[:, :, 1].reshape(parts, groups * CAP, feat)
    partial_out, partial_grad, term = expert_math(inputs, cotangents, gate_full, up_full, down_full)
    summed = lax.psum_scatter(
        term.astype(jnp.bfloat16), "dp", scatter_dimension=0, tiled=True
    ).astype(jnp.float32)
    grad_gate = summed[:, :hid][None]
    grad_up = summed[:, hid : 2 * hid][None]
    grad_down = summed[:, 2 * hid :][None]
    results = jnp.stack(
        [
            partial_out.reshape(parts, groups, CAP, feat),
            partial_grad.reshape(parts, groups, CAP, feat),
        ],
        axis=2,
    )
    returned = lax.all_to_all(
        results[0].astype(jnp.bfloat16), "expert", split_axis=0, concat_axis=0, tiled=True
    ).astype(jnp.float32)
    combined = jnp.sum(
        returned.reshape(window, SPLIT, 2, CAP, width), axis=1, keepdims=True
    ).astype(jnp.bfloat16)
    weighted = select * slot_gate[None, :, :]
    layer_out = jnp.einsum(
        "tec,ehcf->thf", weighted, combined[:, :, 0].astype(jnp.float32), precision=HIGH
    )
    token_grad = jnp.einsum(
        "tec,ehcf->thf", select, combined[:, :, 1].astype(jnp.float32), precision=HIGH
    )
    return (
        layer_out.reshape(tok_rows, width).astype(jnp.bfloat16),
        token_grad.reshape(tok_rows, width).astype(jnp.bfloat16),
        grad_gate,
        grad_up,
        grad_down,
    )


def solution(mesh):
    return jax.shard_map(
        per_device,
        mesh=mesh,
        in_specs=(
            P(("dp", "expert"), None),
            P(("dp", "expert"), None),
            P(("dp", "expert"), None),
            P(("dp", "expert"), None),
            P("expert", "dp", None),
            P("expert", "dp", None),
            P("expert", "dp", None),
        ),
        out_specs=(
            P(("dp", "expert"), None),
            P(("dp", "expert"), None),
            P("expert", "dp", None),
            P("expert", "dp", None),
            P("expert", "dp", None),
        ),
        check_vma=False,
    )
```

```python
import jax
import jax.numpy as jnp
from jax import lax
from jax.sharding import Mesh
from jax.sharding import PartitionSpec as P

SPLIT = 16
CAP = 4


SCALE = 2.0 ** (-16)
HIGH = lax.Precision.HIGHEST
TOK = ("dp", "ex", "ez", "ec")


def routing(ids, gates, window, capacity):
    wanted = jnp.arange(window, dtype=jnp.int32)
    hits = ids[:, :, None] == wanted[None, None, :]
    member = jnp.any(hits, axis=1)
    weight = jnp.sum(jnp.where(hits, gates[:, :, None], 0), axis=1).astype(jnp.float32) * SCALE
    rank = jnp.cumsum(member.astype(jnp.int32), axis=0) - 1
    slots = jnp.arange(capacity, dtype=jnp.int32)
    pick = jnp.logical_and(member[:, :, None], rank[:, :, None] == slots[None, None, :])
    select = jnp.where(pick, 1.0, 0.0).astype(jnp.float32)
    slot_gate = jnp.sum(select * weight[:, :, None], axis=0)
    return (select, slot_gate)


def expert_math(inputs, cotangents, w_all, hid):
    gate_w = w_all[:, :hid]
    up_w = w_all[:, hid : 2 * hid]
    down_w = w_all[:, 2 * hid :]
    f32 = jnp.float32
    gate_pre = jnp.dot(inputs, gate_w, preferred_element_type=f32)
    up_pre = jnp.dot(inputs, up_w, preferred_element_type=f32)
    sig = jax.nn.sigmoid(gate_pre)
    act = gate_pre * sig
    hidden = (act * up_pre).astype(jnp.bfloat16)
    partial_out = lax.dot_general(hidden, down_w, (((1,), (1,)), ((), ())), preferred_element_type=f32)
    d_hidden = jnp.dot(cotangents, down_w, preferred_element_type=f32)
    d_gate = (d_hidden * up_pre * sig * (1.0 + gate_pre * (1.0 - sig))).astype(jnp.bfloat16)
    d_up = (d_hidden * act).astype(jnp.bfloat16)
    partial_grad = lax.dot_general(
        d_gate, gate_w, (((1,), (1,)), ((), ())), preferred_element_type=f32
    ) + lax.dot_general(d_up, up_w, (((1,), (1,)), ((), ())), preferred_element_type=f32)
    tn = (((0,), (0,)), ((), ()))
    term = jnp.concatenate(
        [
            lax.dot_general(inputs, d_gate, tn, preferred_element_type=f32),
            lax.dot_general(inputs, d_up, tn, preferred_element_type=f32),
            lax.dot_general(cotangents, hidden, tn, preferred_element_type=f32),
        ],
        axis=1,
    )
    return (partial_out, partial_grad, term)


def per_device(tokens, out_cotangent, expert_ids, gate_fixed, w_gate, w_up, w_down):
    tok_rows, width = tokens.shape
    window = lax.axis_size("ex")
    hsplit = lax.axis_size("ez") * lax.axis_size("ec")
    hid = w_gate.shape[2]
    select, slot_gate = routing(expert_ids, gate_fixed, window, CAP)
    select_b = select.astype(jnp.bfloat16)
    slot_tokens = jnp.einsum(
        "tec,tf->ecf", select_b, tokens, preferred_element_type=jnp.float32
    ).astype(jnp.bfloat16)
    picked = jnp.einsum("tec,tf->ecf", select_b, out_cotangent, preferred_element_type=jnp.float32)
    slot_cot = (picked * slot_gate[:, :, None]).astype(jnp.bfloat16)
    payload = jnp.stack([slot_tokens, slot_cot], axis=1)
    w_loc = jnp.concatenate([w_gate[0], w_up[0], w_down[0]], axis=1)
    w_all = lax.all_gather(w_loc, "dp", axis=0, tiled=False)
    w_all = w_all.reshape(-1, 3 * hid)
    by_x = lax.all_to_all(payload, "ex", split_axis=0, concat_axis=0, tiled=True)
    arrived = lax.all_gather(by_x, ("ez", "ec"), axis=0, tiled=False)
    inputs = arrived[:, :, 0].reshape(hsplit * window * CAP, width)
    cotangents = arrived[:, :, 1].reshape(hsplit * window * CAP, width)
    partial_out, partial_grad, term = expert_math(inputs, cotangents, w_all, hid)
    summed = lax.psum_scatter(
        term.astype(jnp.bfloat16), "dp", scatter_dimension=0, tiled=True
    ).astype(jnp.float32)
    grad_gate = summed[:, :hid][None]
    grad_up = summed[:, hid : 2 * hid][None]
    grad_down = summed[:, 2 * hid :][None]
    results = jnp.stack(
        [
            partial_out.reshape(hsplit, window, CAP, width),
            partial_grad.reshape(hsplit, window, CAP, width),
        ],
        axis=2,
    ).astype(jnp.bfloat16)
    r2 = results.reshape(-1, 2, window * 2 * CAP * width)
    half = lax.psum_scatter(r2, "ec", scatter_dimension=1, tiled=True)
    reduced = lax.psum_scatter(half.reshape(-1, 256), "ez", scatter_dimension=0, tiled=True)
    reduced = reduced.reshape(window, 2, CAP, width)
    combined = lax.all_to_all(reduced, "ex", split_axis=0, concat_axis=0, tiled=True)
    combined = combined.astype(jnp.float32)
    weighted = select * slot_gate[None, :, :]
    layer_out = jnp.einsum("tec,ecf->tf", weighted, combined[:, 0], precision=HIGH)
    token_grad = jnp.einsum("tec,ecf->tf", select, combined[:, 1], precision=HIGH)
    return (
        layer_out.astype(jnp.bfloat16),
        token_grad.astype(jnp.bfloat16),
        grad_gate,
        grad_up,
        grad_down,
    )


def solution(mesh):
    n_dp = mesh.shape["dp"]
    n_exp = mesh.shape["expert"]
    devices = mesh.devices.reshape(n_dp, n_exp // SPLIT, SPLIT // 2, 2)
    grid = Mesh(devices, ("dp", "ex", "ez", "ec"))
    tok = P(TOK, None)
    wsp = P(("ex", "ez", "ec"), "dp", None)
    return jax.shard_map(
        per_device,
        mesh=grid,
        in_specs=(tok, tok, tok, tok, wsp, wsp, wsp),
        out_specs=(tok, tok, wsp, wsp, wsp),
        check_vma=False,
    )
```

```python
import jax
import jax.numpy as jnp
from jax import lax
from jax.sharding import Mesh
from jax.sharding import PartitionSpec as P

SPLIT = 16
CAP = 4


SCALE = 2.0 ** (-16)
HIGH = lax.Precision.HIGHEST
TOK = ("dp", "ex", "ez", "ec")


def routing(ids, gates, window, capacity):
    wanted = jnp.arange(window, dtype=jnp.int32)
    hits = ids[:, :, None] == wanted[None, None, :]
    member = jnp.any(hits, axis=1)
    weight = jnp.sum(jnp.where(hits, gates[:, :, None], 0), axis=1).astype(jnp.float32) * SCALE
    rank = jnp.cumsum(member.astype(jnp.int32), axis=0) - 1
    slots = jnp.arange(capacity, dtype=jnp.int32)
    pick = jnp.logical_and(member[:, :, None], rank[:, :, None] == slots[None, None, :])
    select = jnp.where(pick, 1.0, 0.0).astype(jnp.float32)
    slot_gate = jnp.sum(select * weight[:, :, None], axis=0)
    return (select, slot_gate)


def _shift(n, k):
    return [(i, (i + k) % n) for i in range(n)]


def ring_gather(piece, axis):
    n = lax.axis_size(axis)
    me = lax.axis_index(axis)
    fw = piece
    bw = piece
    ahead = []
    behind = []
    for step in range(n // 2):
        fw = lax.ppermute(fw, axis, _shift(n, 1))
        ahead.append(fw)
        if step < (n - 1) // 2:
            bw = lax.ppermute(bw, axis, _shift(n, -1))
            behind.append(bw)
    rot = jnp.stack([piece] + ahead + behind[::-1], axis=0)
    rev = rot[::-1]
    doubled = jnp.concatenate([rev, rev], axis=0)
    return lax.dynamic_slice_in_dim(doubled, (n - 1 - me) % n, n, axis=0)


def ring_reduce_scatter(full, axis):
    n = lax.axis_size(axis)
    me = lax.axis_index(axis)
    rows = full.shape[0] // n
    cols = full.shape[1] // 2
    chunks = full.reshape(n, rows, full.shape[1])
    left = chunks[:, :, :cols]
    right = chunks[:, :, cols:]

    def pick(part, k):
        return lax.dynamic_index_in_dim(part, k % n, axis=0, keepdims=False).astype(jnp.float32)

    acc_f = pick(left, me - 1)
    acc_b = pick(right, me + 1)
    for step in range(n - 1):
        got_f = lax.ppermute(acc_f.astype(jnp.bfloat16), axis, _shift(n, 1))
        got_b = lax.ppermute(acc_b.astype(jnp.bfloat16), axis, _shift(n, -1))
        acc_f = got_f.astype(jnp.float32) + pick(left, me - 2 - step)
        acc_b = got_b.astype(jnp.float32) + pick(right, me + 2 + step)
    return jnp.concatenate([acc_f, acc_b], axis=1)


def expert_math(inputs, cotangents, w_all, hid):
    gate_w = w_all[:, :hid]
    up_w = w_all[:, hid : 2 * hid]
    down_w = w_all[:, 2 * hid :]
    f32 = jnp.float32
    gate_pre = jnp.dot(inputs, gate_w, preferred_element_type=f32)
    up_pre = jnp.dot(inputs, up_w, preferred_element_type=f32)
    sig = jax.nn.sigmoid(gate_pre)
    act = gate_pre * sig
    hidden = (act * up_pre).astype(jnp.bfloat16)
    partial_out = lax.dot_general(hidden, down_w, (((1,), (1,)), ((), ())), preferred_element_type=f32)
    d_hidden = jnp.dot(cotangents, down_w, preferred_element_type=f32)
    d_gate = (d_hidden * up_pre * sig * (1.0 + gate_pre * (1.0 - sig))).astype(jnp.bfloat16)
    d_up = (d_hidden * act).astype(jnp.bfloat16)
    partial_grad = lax.dot_general(
        d_gate, gate_w, (((1,), (1,)), ((), ())), preferred_element_type=f32
    ) + lax.dot_general(d_up, up_w, (((1,), (1,)), ((), ())), preferred_element_type=f32)
    tn = (((0,), (0,)), ((), ()))
    term = jnp.concatenate(
        [
            lax.dot_general(inputs, d_gate, tn, preferred_element_type=f32),
            lax.dot_general(inputs, d_up, tn, preferred_element_type=f32),
            lax.dot_general(cotangents, hidden, tn, preferred_element_type=f32),
        ],
        axis=1,
    )
    return (partial_out, partial_grad, term)


def per_device(tokens, out_cotangent, expert_ids, gate_fixed, w_gate, w_up, w_down):
    tok_rows, width = tokens.shape
    window = lax.axis_size("ex")
    hsplit = lax.axis_size("ez") * lax.axis_size("ec")
    hid = w_gate.shape[2]
    select, slot_gate = routing(expert_ids, gate_fixed, window, CAP)
    select_b = select.astype(jnp.bfloat16)
    slot_tokens = jnp.einsum(
        "tec,tf->ecf", select_b, tokens, preferred_element_type=jnp.float32
    ).astype(jnp.bfloat16)
    picked = jnp.einsum("tec,tf->ecf", select_b, out_cotangent, preferred_element_type=jnp.float32)
    slot_cot = (picked * slot_gate[:, :, None]).astype(jnp.bfloat16)
    payload = jnp.stack([slot_tokens, slot_cot], axis=1)
    w_loc = jnp.concatenate([w_gate[0], w_up[0], w_down[0]], axis=1)
    w_all = ring_gather(w_loc, "dp").reshape(-1, 3 * hid)
    by_x = lax.all_to_all(payload, "ex", split_axis=0, concat_axis=0, tiled=True)
    arrived = lax.all_gather(by_x, ("ez", "ec"), axis=0, tiled=False)
    inputs = arrived[:, :, 0].reshape(hsplit * window * CAP, width)
    cotangents = arrived[:, :, 1].reshape(hsplit * window * CAP, width)
    partial_out, partial_grad, term = expert_math(inputs, cotangents, w_all, hid)
    summed = ring_reduce_scatter(term.astype(jnp.bfloat16), "dp")
    grad_gate = summed[:, :hid][None]
    grad_up = summed[:, hid : 2 * hid][None]
    grad_down = summed[:, 2 * hid :][None]
    results = jnp.stack(
        [
            partial_out.reshape(hsplit, window, CAP, width),
            partial_grad.reshape(hsplit, window, CAP, width),
        ],
        axis=2,
    ).astype(jnp.bfloat16)
    r2 = results.reshape(-1, 2, window * 2 * CAP * width)
    half = lax.psum_scatter(r2, "ec", scatter_dimension=1, tiled=True)
    reduced = lax.psum_scatter(half.reshape(-1, 256), "ez", scatter_dimension=0, tiled=True)
    reduced = reduced.reshape(window, 2, CAP, width)
    combined = lax.all_to_all(reduced, "ex", split_axis=0, concat_axis=0, tiled=True)
    combined = combined.astype(jnp.float32)
    weighted = select * slot_gate[None, :, :]
    layer_out = jnp.einsum("tec,ecf->tf", weighted, combined[:, 0], precision=HIGH)
    token_grad = jnp.einsum("tec,ecf->tf", select, combined[:, 1], precision=HIGH)
    return (
        layer_out.astype(jnp.bfloat16),
        token_grad.astype(jnp.bfloat16),
        grad_gate,
        grad_up,
        grad_down,
    )


def solution(mesh):
    n_dp = mesh.shape["dp"]
    n_exp = mesh.shape["expert"]
    devices = mesh.devices.reshape(n_dp, n_exp // SPLIT, SPLIT // 2, 2)
    grid = Mesh(devices, ("dp", "ex", "ez", "ec"))
    tok = P(TOK, None)
    wsp = P(("ex", "ez", "ec"), "dp", None)
    return jax.shard_map(
        per_device,
        mesh=grid,
        in_specs=(tok, tok, tok, tok, wsp, wsp, wsp),
        out_specs=(tok, tok, wsp, wsp, wsp),
        check_vma=False,
    )
```

```python
import jax
import jax.numpy as jnp
from jax import lax
from jax.sharding import Mesh
from jax.sharding import PartitionSpec as P

SPLIT = 16
CAP = 4


SCALE = 2.0 ** (-16)
HIGH = lax.Precision.HIGHEST


def routing(ids, gates, window, capacity):
    wanted = jnp.arange(window, dtype=jnp.int32)
    hits = ids[:, :, None] == wanted[None, None, :]
    member = jnp.any(hits, axis=1)
    weight = jnp.sum(jnp.where(hits, gates[:, :, None], 0), axis=1).astype(jnp.float32) * SCALE
    rank = jnp.cumsum(member.astype(jnp.int32), axis=0) - 1
    slots = jnp.arange(capacity, dtype=jnp.int32)
    pick = jnp.logical_and(member[:, :, None], rank[:, :, None] == slots[None, None, :])
    select = jnp.where(pick, 1.0, 0.0).astype(jnp.float32)
    slot_gate = jnp.sum(select * weight[:, :, None], axis=0)
    return (select, slot_gate)


def expert_math(inputs, cotangents, gate_w, up_w, down_w):
    gate_pre = jnp.einsum("prf,pfh->rh", inputs, gate_w, preferred_element_type=jnp.float32)
    up_pre = jnp.einsum("prf,pfh->rh", inputs, up_w, preferred_element_type=jnp.float32)
    sig = jax.nn.sigmoid(gate_pre)
    act = gate_pre * sig
    hidden = (act * up_pre).astype(jnp.bfloat16)
    partial_out = jnp.einsum("rh,pfh->prf", hidden, down_w, preferred_element_type=jnp.float32)
    d_hidden = jnp.einsum("prf,pfh->rh", cotangents, down_w, preferred_element_type=jnp.float32)
    d_gate = (d_hidden * up_pre * sig * (1.0 + gate_pre * (1.0 - sig))).astype(jnp.bfloat16)
    d_up = (d_hidden * act).astype(jnp.bfloat16)
    partial_grad = jnp.einsum(
        "rh,pfh->prf", d_gate, gate_w, preferred_element_type=jnp.float32
    ) + jnp.einsum("rh,pfh->prf", d_up, up_w, preferred_element_type=jnp.float32)
    term = jnp.concatenate(
        [
            jnp.einsum("prf,rh->pfh", inputs, d_gate, preferred_element_type=jnp.float32),
            jnp.einsum("prf,rh->pfh", inputs, d_up, preferred_element_type=jnp.float32),
            jnp.einsum("prf,rh->pfh", cotangents, hidden, preferred_element_type=jnp.float32),
        ],
        axis=2,
    )
    return (partial_out, partial_grad, term.reshape(-1, term.shape[2]))


def per_device(tokens, out_cotangent, expert_ids, gate_fixed, w_gate, w_up, w_down):
    tok_rows, width = tokens.shape
    window = lax.axis_size("ex")
    zsize = lax.axis_size("ez")
    hid = w_gate.shape[2]
    f32 = jnp.float32
    select, slot_gate = routing(expert_ids, gate_fixed, window, CAP)
    select_b = select.astype(jnp.bfloat16)
    slot_tokens = jnp.einsum("tec,tf->ecf", select_b, tokens, preferred_element_type=f32).astype(
        jnp.bfloat16
    )
    picked = jnp.einsum("tec,tf->ecf", select_b, out_cotangent, preferred_element_type=f32)
    slot_cot = (picked * slot_gate[:, :, None]).astype(jnp.bfloat16)
    payload = jnp.stack([slot_tokens, slot_cot], axis=1)
    w_loc = jnp.concatenate([w_gate[0], w_up[0], w_down[0]], axis=1)
    w_all = lax.all_gather(w_loc, "dp", axis=0, tiled=False).reshape(-1, 3 * hid)
    gate_full = w_all[None, :, :hid]
    up_full = w_all[None, :, hid : 2 * hid]
    down_full = w_all[None, :, 2 * hid :]
    outgoing = jnp.broadcast_to(payload[:, None], (window, zsize, 2, CAP, width)).reshape(
        window * zsize, 2, CAP, width
    )
    mine = lax.all_to_all(outgoing, ("ex", "ez"), split_axis=0, concat_axis=0, tiled=True)
    partner = lax.ppermute(mine, "ec", [(0, 1), (1, 0)])
    arrived = jnp.stack([mine, partner], axis=0)
    inputs = arrived[:, :, 0].reshape(1, -1, width)
    cotangents = arrived[:, :, 1].reshape(1, -1, width)
    partial_out, partial_grad, term = expert_math(inputs, cotangents, gate_full, up_full, down_full)
    summed = lax.psum_scatter(
        term.astype(jnp.bfloat16), "dp", scatter_dimension=0, tiled=True
    ).astype(f32)
    grad_gate = summed[:, :hid][None]
    grad_up = summed[:, hid : 2 * hid][None]
    grad_down = summed[:, 2 * hid :][None]
    results = jnp.stack(
        [
            partial_out.reshape(2, window * zsize, CAP, width),
            partial_grad.reshape(2, window * zsize, CAP, width),
        ],
        axis=2,
    )
    back = lax.ppermute(results[1].astype(jnp.bfloat16), "ec", [(0, 1), (1, 0)])
    pair = (results[0] + back.astype(f32)).astype(jnp.bfloat16)
    returned = lax.all_to_all(pair, ("ex", "ez"), split_axis=0, concat_axis=0, tiled=True)
    combined = jnp.sum(
        returned.reshape(window, zsize, 2, CAP, width).astype(f32), axis=1
    ).astype(jnp.bfloat16).astype(f32)
    weighted = select * slot_gate[None, :, :]
    layer_out = jnp.einsum("tec,ecf->tf", weighted, combined[:, 0], precision=HIGH)
    token_grad = jnp.einsum("tec,ecf->tf", select, combined[:, 1], precision=HIGH)
    return (
        layer_out.astype(jnp.bfloat16),
        token_grad.astype(jnp.bfloat16),
        grad_gate,
        grad_up,
        grad_down,
    )


def solution(mesh):
    n_dp = mesh.shape["dp"]
    n_exp = mesh.shape["expert"]
    devices = mesh.devices.reshape(n_dp, n_exp // SPLIT, SPLIT // 2, 2)
    grid = Mesh(devices, ("dp", "ex", "ez", "ec"))
    tok = P(("dp", "ex", "ez", "ec"), None)
    wsp = P(("ex", "ez", "ec"), "dp", None)
    return jax.shard_map(
        per_device,
        mesh=grid,
        in_specs=(tok, tok, tok, tok, wsp, wsp, wsp),
        out_specs=(tok, tok, wsp, wsp, wsp),
        check_vma=False,
    )
```

```python
import jax
import jax.numpy as jnp
from jax import lax
from jax.sharding import Mesh
from jax.sharding import PartitionSpec as P

SPLIT = 16
CAP = 4


SCALE = 2.0 ** (-16)
HIGH = lax.Precision.HIGHEST


def routing(ids, gates, window, capacity):
    wanted = jnp.arange(window, dtype=jnp.int32)
    hits = ids[:, :, None] == wanted[None, None, :]
    member = jnp.any(hits, axis=1)
    weight = jnp.sum(jnp.where(hits, gates[:, :, None], 0), axis=1).astype(jnp.float32) * SCALE
    rank = jnp.cumsum(member.astype(jnp.int32), axis=0) - 1
    slots = jnp.arange(capacity, dtype=jnp.int32)
    pick = jnp.logical_and(member[:, :, None], rank[:, :, None] == slots[None, None, :])
    select = jnp.where(pick, 1.0, 0.0).astype(jnp.float32)
    slot_gate = jnp.sum(select * weight[:, :, None], axis=0)
    return (select, slot_gate)


def expert_math(inputs, cotangents, gate_w, up_w, down_w):
    f32 = jnp.float32
    nt = (((1,), (1,)), ((), ()))
    tn = (((0,), (0,)), ((), ()))
    gate_pre = jnp.dot(inputs, gate_w, preferred_element_type=f32)
    up_pre = jnp.dot(inputs, up_w, preferred_element_type=f32)
    sig = jax.nn.sigmoid(gate_pre)
    act = gate_pre * sig
    hidden = (act * up_pre).astype(jnp.bfloat16)
    partial_out = lax.dot_general(hidden, down_w, nt, preferred_element_type=f32)
    d_hidden = jnp.dot(cotangents, down_w, preferred_element_type=f32)
    d_gate = (d_hidden * up_pre * sig * (1.0 + gate_pre * (1.0 - sig))).astype(jnp.bfloat16)
    d_up = (d_hidden * act).astype(jnp.bfloat16)
    partial_grad = lax.dot_general(d_gate, gate_w, nt, preferred_element_type=f32) + lax.dot_general(
        d_up, up_w, nt, preferred_element_type=f32
    )
    term = jnp.concatenate(
        [
            lax.dot_general(inputs, d_gate, tn, preferred_element_type=f32),
            lax.dot_general(inputs, d_up, tn, preferred_element_type=f32),
            lax.dot_general(cotangents, hidden, tn, preferred_element_type=f32),
        ],
        axis=1,
    )
    return (partial_out, partial_grad, term)


def dispatch(slots, window, zsize):
    cap, width = slots.shape[1], slots.shape[2]
    outgoing = jnp.broadcast_to(slots[:, None], (window, zsize, cap, width)).reshape(
        window * zsize, cap, width
    )
    mine = lax.all_to_all(outgoing, ("ex", "ez"), split_axis=0, concat_axis=0, tiled=True)
    partner = lax.ppermute(mine, "ec", [(0, 1), (1, 0)])
    return jnp.concatenate([mine, partner], axis=0).reshape(-1, width)


def give_back(partial, window, zsize, cap):
    width = partial.shape[1]
    halves = partial.reshape(2, window * zsize, cap, width)
    back = lax.ppermute(halves[1].astype(jnp.bfloat16), "ec", [(0, 1), (1, 0)])
    pair = (halves[0] + back.astype(jnp.float32)).astype(jnp.bfloat16)
    returned = lax.all_to_all(pair, ("ex", "ez"), split_axis=0, concat_axis=0, tiled=True)
    total = jnp.sum(returned.reshape(window, zsize, cap, width).astype(jnp.float32), axis=1)
    return total.astype(jnp.bfloat16).astype(jnp.float32)


def per_device(tokens, out_cotangent, expert_ids, gate_fixed, w_gate, w_up, w_down):
    window = lax.axis_size("ex")
    zsize = lax.axis_size("ez")
    hid = w_gate.shape[2]
    f32 = jnp.float32
    select, slot_gate = routing(expert_ids, gate_fixed, window, CAP)
    select_b = select.astype(jnp.bfloat16)
    slot_tokens = jnp.einsum("tec,tf->ecf", select_b, tokens, preferred_element_type=f32).astype(
        jnp.bfloat16
    )
    picked = jnp.einsum("tec,tf->ecf", select_b, out_cotangent, preferred_element_type=f32)
    slot_cot = (picked * slot_gate[:, :, None]).astype(jnp.bfloat16)
    w_loc = jnp.concatenate([w_gate[0], w_up[0], w_down[0]], axis=1)
    w_all = lax.all_gather(w_loc, "dp", axis=0, tiled=False).reshape(-1, 3 * hid)
    inputs = dispatch(slot_tokens, window, zsize)
    cotangents = dispatch(slot_cot, window, zsize)
    partial_out, partial_grad, term = expert_math(
        inputs, cotangents, w_all[:, :hid], w_all[:, hid : 2 * hid], w_all[:, 2 * hid :]
    )
    summed = lax.psum_scatter(
        term.astype(jnp.bfloat16), "dp", scatter_dimension=0, tiled=True
    ).astype(f32)
    grad_gate = summed[:, :hid][None]
    grad_up = summed[:, hid : 2 * hid][None]
    grad_down = summed[:, 2 * hid :][None]
    out_slots = give_back(partial_out, window, zsize, CAP)
    grad_slots = give_back(partial_grad, window, zsize, CAP)
    weighted = select * slot_gate[None, :, :]
    layer_out = jnp.einsum("tec,ecf->tf", weighted, out_slots, precision=HIGH)
    token_grad = jnp.einsum("tec,ecf->tf", select, grad_slots, precision=HIGH)
    return (
        layer_out.astype(jnp.bfloat16),
        token_grad.astype(jnp.bfloat16),
        grad_gate,
        grad_up,
        grad_down,
    )


def solution(mesh):
    n_dp = mesh.shape["dp"]
    n_exp = mesh.shape["expert"]
    devices = mesh.devices.reshape(n_dp, n_exp // SPLIT, SPLIT // 2, 2)
    grid = Mesh(devices, ("dp", "ex", "ez", "ec"))
    tok = P(("dp", "ex", "ez", "ec"), None)
    wsp = P(("ex", "ez", "ec"), "dp", None)
    return jax.shard_map(
        per_device,
        mesh=grid,
        in_specs=(tok, tok, tok, tok, wsp, wsp, wsp),
        out_specs=(tok, tok, wsp, wsp, wsp),
        check_vma=False,
    )
```

```python
import jax
import jax.numpy as jnp
from jax import lax
from jax.sharding import Mesh
from jax.sharding import PartitionSpec as P

SPLIT = 16
CAP = 4


SCALE = 2.0 ** (-16)
HIGH = lax.Precision.HIGHEST


def routing(ids, gates, window, capacity):
    wanted = jnp.arange(window, dtype=jnp.int32)
    hits = ids[:, :, None] == wanted[None, None, :]
    member = jnp.any(hits, axis=1)
    weight = jnp.sum(jnp.where(hits, gates[:, :, None], 0), axis=1).astype(jnp.float32) * SCALE
    rank = jnp.cumsum(member.astype(jnp.int32), axis=0) - 1
    slots = jnp.arange(capacity, dtype=jnp.int32)
    pick = jnp.logical_and(member[:, :, None], rank[:, :, None] == slots[None, None, :])
    select = jnp.where(pick, 1.0, 0.0).astype(jnp.float32)
    slot_gate = jnp.sum(select * weight[:, :, None], axis=0)
    return (select, slot_gate)


def expert_math(rows, w_all, hid):
    f32 = jnp.float32
    bf16 = jnp.bfloat16
    nt = (((1,), (1,)), ((), ()))
    tn = (((0,), (0,)), ((), ()))
    n = rows.shape[0]
    pre = jnp.dot(rows.reshape(-1, rows.shape[-1]), w_all, preferred_element_type=f32)
    pre = pre.reshape(n, 2, -1, 3 * hid)
    gate_pre = pre[:, 0, :, :hid]
    up_pre = pre[:, 0, :, hid : 2 * hid]
    d_hidden = pre[:, 1, :, 2 * hid :]
    sig = jax.nn.sigmoid(gate_pre)
    act = gate_pre * sig
    hidden = (act * up_pre).astype(bf16)
    d_gate = (d_hidden * up_pre * sig * (1.0 + gate_pre * (1.0 - sig))).astype(bf16)
    d_up = (d_hidden * act).astype(bf16)
    zero = jnp.zeros_like(hidden)
    tok_side = jnp.concatenate([d_gate, d_up, zero], axis=-1)
    cot_side = jnp.concatenate([zero, zero, hidden], axis=-1)
    grad_side = jnp.stack([tok_side, cot_side], axis=1).reshape(-1, 3 * hid)
    out_side = jnp.stack(
        [jnp.concatenate([zero, zero, hidden], axis=-1), jnp.concatenate([d_gate, d_up, zero], axis=-1)],
        axis=1,
    ).reshape(-1, 3 * hid)
    flat = rows.reshape(-1, rows.shape[-1])
    term = lax.dot_general(flat, grad_side, tn, preferred_element_type=f32)
    results = lax.dot_general(out_side, w_all, nt, preferred_element_type=f32)
    return results.reshape(rows.shape), term


def per_device(tokens, out_cotangent, expert_ids, gate_fixed, w_gate, w_up, w_down):
    tok_rows, width = tokens.shape
    window = lax.axis_size("ex")
    zsize = lax.axis_size("ez")
    hid = w_gate.shape[2]
    f32 = jnp.float32
    select, slot_gate = routing(expert_ids, gate_fixed, window, CAP)
    select_b = select.astype(jnp.bfloat16)
    slot_tokens = jnp.einsum("tec,tf->ecf", select_b, tokens, preferred_element_type=f32).astype(
        jnp.bfloat16
    )
    picked = jnp.einsum("tec,tf->ecf", select_b, out_cotangent, preferred_element_type=f32)
    slot_cot = (picked * slot_gate[:, :, None]).astype(jnp.bfloat16)
    payload = jnp.stack([slot_tokens, slot_cot], axis=1)
    w_loc = jnp.concatenate([w_gate[0], w_up[0], w_down[0]], axis=1)
    w_all = lax.all_gather(w_loc, "dp", axis=0, tiled=False).reshape(-1, 3 * hid)
    outgoing = jnp.broadcast_to(payload[:, None], (window, zsize, 2, CAP, width)).reshape(
        window * zsize, 2, CAP, width
    )
    mine = lax.all_to_all(outgoing, ("ex", "ez"), split_axis=0, concat_axis=0, tiled=True)
    partner = lax.ppermute(mine, "ec", [(0, 1), (1, 0)])
    arrived = jnp.concatenate([mine, partner], axis=0)
    results, term = expert_math(arrived, w_all, hid)
    summed = lax.psum_scatter(
        term.astype(jnp.bfloat16), "dp", scatter_dimension=0, tiled=True
    ).astype(f32)
    grad_gate = summed[:, :hid][None]
    grad_up = summed[:, hid : 2 * hid][None]
    grad_down = summed[:, 2 * hid :][None]
    halves = results.reshape(2, window * zsize, 2, CAP, width)
    back = lax.ppermute(halves[1].astype(jnp.bfloat16), "ec", [(0, 1), (1, 0)])
    pair = (halves[0] + back.astype(f32)).astype(jnp.bfloat16)
    returned = lax.all_to_all(pair, ("ex", "ez"), split_axis=0, concat_axis=0, tiled=True)
    combined = jnp.sum(
        returned.reshape(window, zsize, 2, CAP, width).astype(f32), axis=1
    ).astype(jnp.bfloat16).astype(f32)
    weighted = select * slot_gate[None, :, :]
    layer_out = jnp.einsum("tec,ecf->tf", weighted, combined[:, 0], precision=HIGH)
    token_grad = jnp.einsum("tec,ecf->tf", select, combined[:, 1], precision=HIGH)
    return (
        layer_out.astype(jnp.bfloat16),
        token_grad.astype(jnp.bfloat16),
        grad_gate,
        grad_up,
        grad_down,
    )


def solution(mesh):
    n_dp = mesh.shape["dp"]
    n_exp = mesh.shape["expert"]
    devices = mesh.devices.reshape(n_dp, n_exp // SPLIT, SPLIT // 2, 2)
    grid = Mesh(devices, ("dp", "ex", "ez", "ec"))
    tok = P(("dp", "ex", "ez", "ec"), None)
    wsp = P(("ex", "ez", "ec"), "dp", None)
    return jax.shard_map(
        per_device,
        mesh=grid,
        in_specs=(tok, tok, tok, tok, wsp, wsp, wsp),
        out_specs=(tok, tok, wsp, wsp, wsp),
        check_vma=False,
    )
```

```python
import jax
import jax.numpy as jnp
from jax import lax
from jax.sharding import Mesh
from jax.sharding import PartitionSpec as P

SPLIT = 16
CAP = 4


SCALE = 2.0 ** (-16)
HIGH = lax.Precision.HIGHEST


def routing(ids, gates, window, capacity):
    wanted = jnp.arange(window, dtype=jnp.int32)
    hits = ids[:, :, None] == wanted[None, None, :]
    member = jnp.any(hits, axis=1)
    weight = jnp.sum(jnp.where(hits, gates[:, :, None], 0), axis=1).astype(jnp.float32) * SCALE
    rank = jnp.cumsum(member.astype(jnp.int32), axis=0) - 1
    slots = jnp.arange(capacity, dtype=jnp.int32)
    pick = jnp.logical_and(member[:, :, None], rank[:, :, None] == slots[None, None, :])
    select = jnp.where(pick, 1.0, 0.0).astype(jnp.float32)
    slot_gate = jnp.sum(select * weight[:, :, None], axis=0)
    return (select, slot_gate)


def expert_math(rows, w_all, hid):
    f32 = jnp.float32
    bf16 = jnp.bfloat16
    nt = (((1,), (1,)), ((), ()))
    tn = (((0,), (0,)), ((), ()))
    n = rows.shape[0]
    flat = rows.reshape(-1, rows.shape[-1])
    pre = jnp.dot(flat, w_all, preferred_element_type=f32)
    pre = pre.reshape(n, 2, -1, 3 * hid)
    gate_pre = pre[:, 0, :, :hid]
    up_pre = pre[:, 0, :, hid : 2 * hid]
    d_hidden = pre[:, 1, :, 2 * hid :]
    sig = jax.nn.sigmoid(gate_pre)
    act = gate_pre * sig
    hidden = (act * up_pre).astype(bf16)
    d_gate = (d_hidden * up_pre * sig * (1.0 + gate_pre * (1.0 - sig))).astype(bf16)
    d_up = (d_hidden * act).astype(bf16)
    zero = jnp.zeros_like(hidden)
    tok_side = jnp.concatenate([d_gate, d_up, zero], axis=-1)
    cot_side = jnp.concatenate([zero, zero, hidden], axis=-1)
    grad_side = jnp.stack([tok_side, cot_side], axis=1).reshape(-1, 3 * hid)
    out_side = jnp.stack(
        [jnp.concatenate([zero, zero, hidden], axis=-1), jnp.concatenate([d_gate, d_up, zero], axis=-1)],
        axis=1,
    ).reshape(-1, 3 * hid)
    term = lax.dot_general(flat, grad_side, tn, preferred_element_type=f32)
    results = lax.dot_general(out_side, w_all, nt, preferred_element_type=f32)
    return results, term


def per_device(tokens, out_cotangent, expert_ids, gate_fixed, w_gate, w_up, w_down):
    tok_rows, width = tokens.shape
    window = lax.axis_size("ex")
    zsize = lax.axis_size("ez")
    hid = w_gate.shape[2]
    f32 = jnp.float32
    select, slot_gate = routing(expert_ids, gate_fixed, window, CAP)
    select_b = select.astype(jnp.bfloat16)
    slot_tokens = jnp.einsum("tec,tf->ecf", select_b, tokens, preferred_element_type=f32).astype(
        jnp.bfloat16
    )
    picked = jnp.einsum("tec,tf->ecf", select_b, out_cotangent, preferred_element_type=f32)
    slot_cot = (picked * slot_gate[:, :, None]).astype(jnp.bfloat16)
    payload = jnp.concatenate([slot_tokens, slot_cot], axis=1)
    w_loc = jnp.concatenate([w_gate[0], w_up[0], w_down[0]], axis=1)
    w_all = lax.all_gather(w_loc, "dp", axis=0, tiled=False).reshape(-1, 3 * hid)
    outgoing = jnp.broadcast_to(payload[:, None], (window, zsize, 2 * CAP, width)).reshape(
        window * zsize, 2 * CAP, width
    )
    mine = lax.all_to_all(outgoing, ("ex", "ez"), split_axis=0, concat_axis=0, tiled=True)
    partner = lax.ppermute(mine, "ec", [(0, 1), (1, 0)])
    arrived = jnp.concatenate([mine, partner], axis=0)
    results, term = expert_math(arrived, w_all, hid)
    summed = lax.psum_scatter(
        term.astype(jnp.bfloat16), "dp", scatter_dimension=0, tiled=True
    ).astype(f32)
    grad_gate = summed[:, :hid][None]
    grad_up = summed[:, hid : 2 * hid][None]
    grad_down = summed[:, 2 * hid :][None]
    halves = results.reshape(2, window * zsize, 2 * CAP, width)
    back = lax.ppermute(halves[1].astype(jnp.bfloat16), "ec", [(0, 1), (1, 0)])
    pair = (halves[0] + back.astype(f32)).astype(jnp.bfloat16)
    returned = lax.all_to_all(pair, ("ex", "ez"), split_axis=0, concat_axis=0, tiled=True)
    combined = jnp.sum(
        returned.reshape(window, zsize, 2 * CAP, width).astype(f32), axis=1
    ).astype(jnp.bfloat16).astype(f32).reshape(window, 2, CAP, width)
    weighted = select * slot_gate[None, :, :]
    layer_out = jnp.einsum("tec,ecf->tf", weighted, combined[:, 0], precision=HIGH)
    token_grad = jnp.einsum("tec,ecf->tf", select, combined[:, 1], precision=HIGH)
    return (
        layer_out.astype(jnp.bfloat16),
        token_grad.astype(jnp.bfloat16),
        grad_gate,
        grad_up,
        grad_down,
    )


def solution(mesh):
    n_dp = mesh.shape["dp"]
    n_exp = mesh.shape["expert"]
    devices = mesh.devices.reshape(n_dp, n_exp // SPLIT, SPLIT // 2, 2)
    grid = Mesh(devices, ("dp", "ex", "ez", "ec"))
    tok = P(("dp", "ex", "ez", "ec"), None)
    wsp = P(("ex", "ez", "ec"), "dp", None)
    return jax.shard_map(
        per_device,
        mesh=grid,
        in_specs=(tok, tok, tok, tok, wsp, wsp, wsp),
        out_specs=(tok, tok, wsp, wsp, wsp),
        check_vma=False,
    )
```

```python
import jax
import jax.numpy as jnp
from jax import lax
from jax.sharding import Mesh
from jax.sharding import PartitionSpec as P

SPLIT = 16
CAP = 4


SCALE = 2.0 ** (-16)
HIGH = lax.Precision.HIGHEST


def routing(ids, gates, window, capacity):
    wanted = jnp.arange(window, dtype=jnp.int32)
    hits = ids[:, :, None] == wanted[None, None, :]
    member = jnp.any(hits, axis=1)
    weight = jnp.sum(jnp.where(hits, gates[:, :, None], 0), axis=1).astype(jnp.float32) * SCALE
    rank = jnp.cumsum(member.astype(jnp.int32), axis=0) - 1
    slots = jnp.arange(capacity, dtype=jnp.int32)
    pick = jnp.logical_and(member[:, :, None], rank[:, :, None] == slots[None, None, :])
    select = jnp.where(pick, 1.0, 0.0).astype(jnp.float32)
    slot_gate = jnp.sum(select * weight[:, :, None], axis=0)
    return (select, slot_gate)


def expert_math(mine, partner, w_all, hid):
    f32 = jnp.float32
    bf16 = jnp.bfloat16
    nt = (((1,), (1,)), ((), ()))
    tn = (((0,), (0,)), ((), ()))
    n = mine.shape[0]
    flat_m = mine.reshape(-1, mine.shape[-1])
    flat_p = partner.reshape(-1, partner.shape[-1])
    pre_m = jnp.dot(flat_m, w_all, preferred_element_type=f32)
    pre_p = jnp.dot(flat_p, w_all, preferred_element_type=f32)
    pre = jnp.stack([pre_m, pre_p], axis=0).reshape(2, n, 2, -1, 3 * hid)
    gate_pre = pre[:, :, 0, :, :hid]
    up_pre = pre[:, :, 0, :, hid : 2 * hid]
    d_hidden = pre[:, :, 1, :, 2 * hid :]
    sig = jax.nn.sigmoid(gate_pre)
    act = gate_pre * sig
    hidden = (act * up_pre).astype(bf16)
    d_gate = (d_hidden * up_pre * sig * (1.0 + gate_pre * (1.0 - sig))).astype(bf16)
    d_up = (d_hidden * act).astype(bf16)
    zero = jnp.zeros_like(hidden)
    tok_side = jnp.concatenate([d_gate, d_up, zero], axis=-1)
    cot_side = jnp.concatenate([zero, zero, hidden], axis=-1)
    grad_side = jnp.stack([tok_side, cot_side], axis=2).reshape(2, -1, 3 * hid)
    out_side = jnp.stack([cot_side, tok_side], axis=2).reshape(2, -1, 3 * hid)
    res_p = lax.dot_general(out_side[1], w_all, nt, preferred_element_type=f32)
    res_m = lax.dot_general(out_side[0], w_all, nt, preferred_element_type=f32)
    term = lax.dot_general(flat_m, grad_side[0], tn, preferred_element_type=f32) + lax.dot_general(
        flat_p, grad_side[1], tn, preferred_element_type=f32
    )
    return res_m, res_p, term


def per_device(tokens, out_cotangent, expert_ids, gate_fixed, w_gate, w_up, w_down):
    tok_rows, width = tokens.shape
    window = lax.axis_size("ex")
    zsize = lax.axis_size("ez")
    hid = w_gate.shape[2]
    f32 = jnp.float32
    select, slot_gate = routing(expert_ids, gate_fixed, window, CAP)
    select_b = select.astype(jnp.bfloat16)
    slot_tokens = jnp.einsum("tec,tf->ecf", select_b, tokens, preferred_element_type=f32).astype(
        jnp.bfloat16
    )
    picked = jnp.einsum("tec,tf->ecf", select_b, out_cotangent, preferred_element_type=f32)
    slot_cot = (picked * slot_gate[:, :, None]).astype(jnp.bfloat16)
    payload = jnp.concatenate([slot_tokens, slot_cot], axis=1)
    w_loc = jnp.concatenate([w_gate[0], w_up[0], w_down[0]], axis=1)
    w_all = lax.all_gather(w_loc, "dp", axis=0, tiled=False).reshape(-1, 3 * hid)
    outgoing = jnp.broadcast_to(payload[:, None], (window, zsize, 2 * CAP, width)).reshape(
        window * zsize, 2 * CAP, width
    )
    mine = lax.all_to_all(outgoing, ("ex", "ez"), split_axis=0, concat_axis=0, tiled=True)
    partner = lax.ppermute(mine, "ec", [(0, 1), (1, 0)])
    res_m, res_p, term = expert_math(mine, partner, w_all, hid)
    summed = lax.psum_scatter(
        term.astype(jnp.bfloat16), "dp", scatter_dimension=0, tiled=True
    ).astype(f32)
    grad_gate = summed[:, :hid][None]
    grad_up = summed[:, hid : 2 * hid][None]
    grad_down = summed[:, 2 * hid :][None]
    back = lax.ppermute(res_p.astype(jnp.bfloat16), "ec", [(0, 1), (1, 0)])
    pair = (res_m + back.astype(f32)).astype(jnp.bfloat16).reshape(window * zsize, 2 * CAP, width)
    returned = lax.all_to_all(pair, ("ex", "ez"), split_axis=0, concat_axis=0, tiled=True)
    combined = jnp.sum(
        returned.reshape(window, zsize, 2 * CAP, width).astype(f32), axis=1
    ).astype(jnp.bfloat16).astype(f32).reshape(window, 2, CAP, width)
    weighted = select * slot_gate[None, :, :]
    layer_out = jnp.einsum("tec,ecf->tf", weighted, combined[:, 0], precision=HIGH)
    token_grad = jnp.einsum("tec,ecf->tf", select, combined[:, 1], precision=HIGH)
    return (
        layer_out.astype(jnp.bfloat16),
        token_grad.astype(jnp.bfloat16),
        grad_gate,
        grad_up,
        grad_down,
    )


def solution(mesh):
    n_dp = mesh.shape["dp"]
    n_exp = mesh.shape["expert"]
    devices = mesh.devices.reshape(n_dp, n_exp // SPLIT, SPLIT // 2, 2)
    grid = Mesh(devices, ("dp", "ex", "ez", "ec"))
    tok = P(("dp", "ex", "ez", "ec"), None)
    wsp = P(("ex", "ez", "ec"), "dp", None)
    return jax.shard_map(
        per_device,
        mesh=grid,
        in_specs=(tok, tok, tok, tok, wsp, wsp, wsp),
        out_specs=(tok, tok, wsp, wsp, wsp),
        check_vma=False,
    )
```

```python
import jax
import jax.numpy as jnp
from jax import lax
from jax.sharding import Mesh
from jax.sharding import PartitionSpec as P

SPLIT = 16
CAP = 4


SCALE = 2.0 ** (-16)
HIGH = lax.Precision.HIGHEST


def routing(ids, gates, window, capacity):
    wanted = jnp.arange(window, dtype=jnp.int32)
    hits = ids[:, :, None] == wanted[None, None, :]
    member = jnp.any(hits, axis=1)
    weight = jnp.sum(jnp.where(hits, gates[:, :, None], 0), axis=1).astype(jnp.float32) * SCALE
    rank = jnp.cumsum(member.astype(jnp.int32), axis=0) - 1
    slots = jnp.arange(capacity, dtype=jnp.int32)
    pick = jnp.logical_and(member[:, :, None], rank[:, :, None] == slots[None, None, :])
    select = jnp.where(pick, 1.0, 0.0).astype(jnp.float32)
    slot_gate = jnp.sum(select * weight[:, :, None], axis=0)
    return (select, slot_gate)


def expert_math(mine, w_two, hid):
    f32 = jnp.float32
    bf16 = jnp.bfloat16
    nt = (((1,), (1,)), ((), ()))
    tn = (((0,), (0,)), ((), ()))
    n = mine.shape[0]
    flat = mine.reshape(-1, mine.shape[-1])
    pre = jnp.dot(flat, w_two, preferred_element_type=f32).reshape(n, 2, -1, 2, 3 * hid)
    gate_pre = pre[:, 0, :, :, :hid]
    up_pre = pre[:, 0, :, :, hid : 2 * hid]
    d_hidden = pre[:, 1, :, :, 2 * hid :]
    sig = jax.nn.sigmoid(gate_pre)
    act = gate_pre * sig
    hidden = (act * up_pre).astype(bf16)
    d_gate = (d_hidden * up_pre * sig * (1.0 + gate_pre * (1.0 - sig))).astype(bf16)
    d_up = (d_hidden * act).astype(bf16)
    zero = jnp.zeros_like(hidden)
    tok_side = jnp.concatenate([d_gate, d_up, zero], axis=-1)
    cot_side = jnp.concatenate([zero, zero, hidden], axis=-1)
    grad_side = jnp.stack([tok_side, cot_side], axis=1).reshape(-1, 2 * 3 * hid)
    out_side = jnp.stack([cot_side, tok_side], axis=1).reshape(-1, 2 * 3 * hid)
    results = lax.dot_general(out_side, w_two, nt, preferred_element_type=f32)
    term = lax.dot_general(flat, grad_side, tn, preferred_element_type=f32)
    return results, term.reshape(term.shape[0], 2, 3 * hid)


def per_device(tokens, out_cotangent, expert_ids, gate_fixed, w_gate, w_up, w_down):
    window = lax.axis_size("ex")
    zsize = lax.axis_size("ez")
    hid = w_gate.shape[2]
    f32 = jnp.float32
    core = lax.axis_index("ec")
    swap = [(0, 1), (1, 0)]
    w_loc = jnp.concatenate([w_gate[0], w_up[0], w_down[0]], axis=1)
    w_all = lax.all_gather(w_loc, "dp", axis=0, tiled=False).reshape(-1, 3 * hid)
    w_other = lax.ppermute(w_all, "ec", swap)
    w_pair = jnp.stack([w_all, w_other], axis=1)
    w_pair = jnp.where(core == 0, w_pair, w_pair[:, ::-1])
    w_two = w_pair.reshape(-1, 2 * 3 * hid)
    select, slot_gate = routing(expert_ids, gate_fixed, window, CAP)
    select_b = select.astype(jnp.bfloat16)
    slot_tokens = jnp.einsum("tec,tf->ecf", select_b, tokens, preferred_element_type=f32).astype(
        jnp.bfloat16
    )
    picked = jnp.einsum("tec,tf->ecf", select_b, out_cotangent, preferred_element_type=f32)
    slot_cot = (picked * slot_gate[:, :, None]).astype(jnp.bfloat16)
    payload = jnp.concatenate([slot_tokens, slot_cot], axis=1)
    width = payload.shape[-1]
    outgoing = jnp.broadcast_to(payload[:, None], (window, zsize, 2 * CAP, width)).reshape(
        window * zsize, 2 * CAP, width
    )
    mine = lax.all_to_all(outgoing, ("ex", "ez"), split_axis=0, concat_axis=0, tiled=True)
    results, term = expert_math(mine, w_two, hid)
    own = jnp.where(core == 0, term[:, 0], term[:, 1])
    other = jnp.where(core == 0, term[:, 1], term[:, 0])
    got = lax.ppermute(other.astype(jnp.bfloat16), "ec", swap)
    chip_term = own + got.astype(f32)
    summed = lax.psum_scatter(
        chip_term.astype(jnp.bfloat16), "dp", scatter_dimension=0, tiled=True
    ).astype(f32)
    grad_gate = summed[:, :hid][None]
    grad_up = summed[:, hid : 2 * hid][None]
    grad_down = summed[:, 2 * hid :][None]
    pair = results.astype(jnp.bfloat16).reshape(window * zsize, 2 * CAP, width)
    returned = lax.all_to_all(pair, ("ex", "ez"), split_axis=0, concat_axis=0, tiled=True)
    combined = jnp.sum(
        returned.reshape(window, zsize, 2 * CAP, width).astype(f32), axis=1
    ).astype(jnp.bfloat16).reshape(window, 2, CAP, width)
    weighted = select * slot_gate[None, :, :]
    layer_out = jnp.einsum("tec,ecf->tf", weighted, combined[:, 0].astype(f32), precision=HIGH)
    token_grad = jnp.einsum("tec,ecf->tf", select_b, combined[:, 1], preferred_element_type=f32)
    return (
        layer_out.astype(jnp.bfloat16),
        token_grad.astype(jnp.bfloat16),
        grad_gate,
        grad_up,
        grad_down,
    )


def solution(mesh):
    n_dp = mesh.shape["dp"]
    n_exp = mesh.shape["expert"]
    devices = mesh.devices.reshape(n_dp, n_exp // SPLIT, SPLIT // 2, 2)
    grid = Mesh(devices, ("dp", "ex", "ez", "ec"))
    tok = P(("dp", "ex", "ez", "ec"), None)
    wsp = P(("ex", "ez", "ec"), "dp", None)
    return jax.shard_map(
        per_device,
        mesh=grid,
        in_specs=(tok, tok, tok, tok, wsp, wsp, wsp),
        out_specs=(tok, tok, wsp, wsp, wsp),
        check_vma=False,
    )
```

```python
import jax
import jax.numpy as jnp
from jax import lax
from jax.sharding import Mesh
from jax.sharding import PartitionSpec as P

SPLIT = 16
CAP = 4


SCALE = 2.0 ** (-16)
HIGH = lax.Precision.HIGHEST


def routing(ids, gates, window, capacity):
    wanted = jnp.arange(window, dtype=jnp.int32)
    hits = ids[:, :, None] == wanted[None, None, :]
    member = jnp.any(hits, axis=1)
    weight = jnp.sum(jnp.where(hits, gates[:, :, None], 0), axis=1).astype(jnp.float32) * SCALE
    rank = jnp.cumsum(member.astype(jnp.int32), axis=0) - 1
    slots = jnp.arange(capacity, dtype=jnp.int32)
    pick = jnp.logical_and(member[:, :, None], rank[:, :, None] == slots[None, None, :])
    select = jnp.where(pick, 1.0, 0.0).astype(jnp.float32)
    slot_gate = jnp.sum(select * weight[:, :, None], axis=0)
    return (select, slot_gate)


def expert_math(mine, w_two, hid):
    f32 = jnp.float32
    bf16 = jnp.bfloat16
    nt = (((1,), (1,)), ((), ()))
    tn = (((0,), (0,)), ((), ()))
    n = mine.shape[0]
    flat = mine.reshape(-1, mine.shape[-1])
    pre = jnp.dot(flat, w_two, preferred_element_type=f32).reshape(n, 2, -1, 2, 3 * hid)
    gate_pre = pre[:, 0, :, :, :hid]
    up_pre = pre[:, 0, :, :, hid : 2 * hid]
    d_hidden = pre[:, 1, :, :, 2 * hid :]
    sig = jax.nn.sigmoid(gate_pre)
    act = gate_pre * sig
    hidden = (act * up_pre).astype(bf16)
    d_gate = (d_hidden * up_pre * sig * (1.0 + gate_pre * (1.0 - sig))).astype(bf16)
    d_up = (d_hidden * act).astype(bf16)
    zero = jnp.zeros_like(hidden)
    tok_side = jnp.concatenate([d_gate, d_up, zero], axis=-1)
    cot_side = jnp.concatenate([zero, zero, hidden], axis=-1)
    grad_side = jnp.stack([tok_side, cot_side], axis=1).reshape(-1, 2 * 3 * hid)
    out_side = jnp.stack([cot_side, tok_side], axis=1).reshape(-1, 2 * 3 * hid)
    results = lax.dot_general(out_side, w_two, nt, preferred_element_type=f32)
    term = lax.dot_general(flat, grad_side, tn, preferred_element_type=f32)
    return results, term.reshape(term.shape[0], 2, 3 * hid)


def per_device(tokens, out_cotangent, expert_ids, gate_fixed, w_gate, w_up, w_down):
    window = lax.axis_size("ex")
    zsize = lax.axis_size("ez")
    hid = w_gate.shape[2]
    f32 = jnp.float32
    core = lax.axis_index("ec")
    swap = [(0, 1), (1, 0)]
    w_loc = jnp.concatenate([w_gate[0], w_up[0], w_down[0]], axis=1)
    w_all = lax.all_gather(w_loc, "dp", axis=0, tiled=False).reshape(-1, 3 * hid)
    w_other = lax.ppermute(w_all, "ec", swap)
    w_pair = jnp.stack([w_all, w_other], axis=1)
    w_pair = jnp.where(core == 0, w_pair, w_pair[:, ::-1])
    w_two = w_pair.reshape(-1, 2 * 3 * hid)
    select, slot_gate = routing(expert_ids, gate_fixed, window, CAP)
    select_b = select.astype(jnp.bfloat16)
    slot_tokens = jnp.einsum("tec,tf->ecf", select_b, tokens, preferred_element_type=f32).astype(
        jnp.bfloat16
    )
    picked = jnp.einsum("tec,tf->ecf", select_b, out_cotangent, preferred_element_type=f32)
    slot_cot = (picked * slot_gate[:, :, None]).astype(jnp.bfloat16)
    payload = jnp.concatenate([slot_tokens, slot_cot], axis=1)
    width = payload.shape[-1]
    outgoing = jnp.broadcast_to(payload[:, None], (window, zsize, 2 * CAP, width)).reshape(
        window * zsize, 2 * CAP, width
    )
    mine = lax.all_to_all(outgoing, ("ex", "ez"), split_axis=0, concat_axis=0, tiled=True)
    results, term = expert_math(mine, w_two, hid)
    by_core = jnp.transpose(term, (1, 0, 2)).reshape(-1, 3 * hid)
    summed = lax.psum_scatter(
        by_core.astype(jnp.bfloat16), ("ec", "dp"), scatter_dimension=0, tiled=True
    ).astype(f32)
    grad_gate = summed[:, :hid][None]
    grad_up = summed[:, hid : 2 * hid][None]
    grad_down = summed[:, 2 * hid :][None]
    pair = results.astype(jnp.bfloat16).reshape(window * zsize, 2 * CAP, width)
    returned = lax.all_to_all(pair, ("ex", "ez"), split_axis=0, concat_axis=0, tiled=True)
    combined = jnp.sum(
        returned.reshape(window, zsize, 2 * CAP, width).astype(f32), axis=1
    ).astype(jnp.bfloat16).reshape(window, 2, CAP, width)
    weighted = select * slot_gate[None, :, :]
    layer_out = jnp.einsum("tec,ecf->tf", weighted, combined[:, 0].astype(f32), precision=HIGH)
    token_grad = jnp.einsum("tec,ecf->tf", select_b, combined[:, 1], preferred_element_type=f32)
    return (
        layer_out.astype(jnp.bfloat16),
        token_grad.astype(jnp.bfloat16),
        grad_gate,
        grad_up,
        grad_down,
    )


def solution(mesh):
    n_dp = mesh.shape["dp"]
    n_exp = mesh.shape["expert"]
    devices = mesh.devices.reshape(n_dp, n_exp // SPLIT, SPLIT // 2, 2)
    grid = Mesh(devices, ("dp", "ex", "ez", "ec"))
    tok = P(("dp", "ex", "ez", "ec"), None)
    wsp = P(("ex", "ez", "ec"), "dp", None)
    return jax.shard_map(
        per_device,
        mesh=grid,
        in_specs=(tok, tok, tok, tok, wsp, wsp, wsp),
        out_specs=(tok, tok, wsp, wsp, wsp),
        check_vma=False,
    )
```

```python
import jax
import jax.numpy as jnp
from jax import lax
from jax.sharding import Mesh
from jax.sharding import PartitionSpec as P

SPLIT = 16
CAP = 4


SCALE = 2.0 ** (-16)
HIGH = lax.Precision.HIGHEST


def routing(ids, gates, window, capacity):
    wanted = jnp.arange(window, dtype=jnp.int32)
    hits = ids[:, :, None] == wanted[None, None, :]
    member = jnp.any(hits, axis=1)
    weight = jnp.sum(jnp.where(hits, gates[:, :, None], 0), axis=1).astype(jnp.float32) * SCALE
    rank = jnp.cumsum(member.astype(jnp.int32), axis=0) - 1
    slots = jnp.arange(capacity, dtype=jnp.int32)
    pick = jnp.logical_and(member[:, :, None], rank[:, :, None] == slots[None, None, :])
    select = jnp.where(pick, 1.0, 0.0).astype(jnp.float32)
    slot_gate = jnp.sum(select * weight[:, :, None], axis=0)
    return (select, slot_gate)


def expert_math(mine, w_two, hid):
    f32 = jnp.float32
    bf16 = jnp.bfloat16
    nt = (((1,), (1,)), ((), ()))
    tn = (((0,), (0,)), ((), ()))
    n = mine.shape[0]
    flat = mine.reshape(-1, mine.shape[-1])
    pre = jnp.dot(flat, w_two, preferred_element_type=f32).reshape(n, 2, -1, 2, 3 * hid)
    gate_pre = pre[:, 0, :, :, :hid]
    up_pre = pre[:, 0, :, :, hid : 2 * hid]
    d_hidden = pre[:, 1, :, :, 2 * hid :]
    sig = jax.nn.sigmoid(gate_pre)
    act = gate_pre * sig
    hidden = (act * up_pre).astype(bf16)
    d_gate = (d_hidden * up_pre * sig * (1.0 + gate_pre * (1.0 - sig))).astype(bf16)
    d_up = (d_hidden * act).astype(bf16)
    zero = jnp.zeros_like(hidden)
    tok_side = jnp.concatenate([d_gate, d_up, zero], axis=-1)
    cot_side = jnp.concatenate([zero, zero, hidden], axis=-1)
    grad_side = jnp.stack([tok_side, cot_side], axis=1).reshape(-1, 2 * 3 * hid)
    out_side = jnp.stack([cot_side, tok_side], axis=1).reshape(-1, 2 * 3 * hid)
    results = lax.dot_general(out_side, w_two, nt, preferred_element_type=f32)
    return results, grad_side.reshape(-1, 2, 3 * hid)


def per_device(tokens, out_cotangent, expert_ids, gate_fixed, w_gate, w_up, w_down):
    window = lax.axis_size("ex")
    zsize = lax.axis_size("ez")
    hid = w_gate.shape[2]
    f32 = jnp.float32
    core = lax.axis_index("ec")
    swap = [(0, 1), (1, 0)]
    w_loc = jnp.concatenate([w_gate[0], w_up[0], w_down[0]], axis=1)
    w_all = lax.all_gather(w_loc, "dp", axis=0, tiled=False).reshape(-1, 3 * hid)
    w_other = lax.ppermute(w_all, "ec", swap)
    w_pair = jnp.stack([w_all, w_other], axis=1)
    w_pair = jnp.where(core == 0, w_pair, w_pair[:, ::-1])
    w_two = w_pair.reshape(-1, 2 * 3 * hid)
    select, slot_gate = routing(expert_ids, gate_fixed, window, CAP)
    select_b = select.astype(jnp.bfloat16)
    slot_tokens = jnp.einsum("tec,tf->ecf", select_b, tokens, preferred_element_type=f32).astype(
        jnp.bfloat16
    )
    picked = jnp.einsum("tec,tf->ecf", select_b, out_cotangent, preferred_element_type=f32)
    slot_cot = (picked * slot_gate[:, :, None]).astype(jnp.bfloat16)
    payload = jnp.concatenate([slot_tokens, slot_cot], axis=1)
    width = payload.shape[-1]
    outgoing = jnp.broadcast_to(payload[:, None], (window, zsize, 2 * CAP, width)).reshape(
        window * zsize, 2 * CAP, width
    )
    mine = lax.all_to_all(outgoing, ("ex", "ez"), split_axis=0, concat_axis=0, tiled=True)
    partner = lax.ppermute(mine, "ec", swap)
    results, grad_side = expert_math(mine, w_two, hid)
    own_side = jnp.where(core == 0, grad_side[:, 0], grad_side[:, 1])
    other_side = jnp.where(core == 0, grad_side[:, 1], grad_side[:, 0])
    got_side = lax.ppermute(other_side, "ec", swap)
    tn = (((0,), (0,)), ((), ()))
    chip_term = lax.dot_general(
        mine.reshape(-1, width), own_side, tn, preferred_element_type=f32
    ) + lax.dot_general(partner.reshape(-1, width), got_side, tn, preferred_element_type=f32)
    summed = lax.psum_scatter(
        chip_term.astype(jnp.bfloat16), "dp", scatter_dimension=0, tiled=True
    ).astype(f32)
    grad_gate = summed[:, :hid][None]
    grad_up = summed[:, hid : 2 * hid][None]
    grad_down = summed[:, 2 * hid :][None]
    pair = results.astype(jnp.bfloat16).reshape(window * zsize, 2 * CAP, width)
    returned = lax.all_to_all(pair, ("ex", "ez"), split_axis=0, concat_axis=0, tiled=True)
    combined = jnp.sum(
        returned.reshape(window, zsize, 2 * CAP, width).astype(f32), axis=1
    ).astype(jnp.bfloat16).reshape(window, 2, CAP, width)
    weighted = select * slot_gate[None, :, :]
    layer_out = jnp.einsum("tec,ecf->tf", weighted, combined[:, 0].astype(f32), precision=HIGH)
    token_grad = jnp.einsum("tec,ecf->tf", select_b, combined[:, 1], preferred_element_type=f32)
    return (
        layer_out.astype(jnp.bfloat16),
        token_grad.astype(jnp.bfloat16),
        grad_gate,
        grad_up,
        grad_down,
    )


def solution(mesh):
    n_dp = mesh.shape["dp"]
    n_exp = mesh.shape["expert"]
    devices = mesh.devices.reshape(n_dp, n_exp // SPLIT, SPLIT // 2, 2)
    grid = Mesh(devices, ("dp", "ex", "ez", "ec"))
    tok = P(("dp", "ex", "ez", "ec"), None)
    wsp = P(("ex", "ez", "ec"), "dp", None)
    return jax.shard_map(
        per_device,
        mesh=grid,
        in_specs=(tok, tok, tok, tok, wsp, wsp, wsp),
        out_specs=(tok, tok, wsp, wsp, wsp),
        check_vma=False,
    )
```

```python
import jax
import jax.numpy as jnp
from jax import lax
from jax.sharding import Mesh
from jax.sharding import PartitionSpec as P

SPLIT = 16
CAP = 4


SCALE = 2.0 ** (-16)
HIGH = lax.Precision.HIGHEST


def routing(ids, gates, window, capacity):
    wanted = jnp.arange(window, dtype=jnp.int32)
    hits = ids[:, :, None] == wanted[None, None, :]
    member = jnp.any(hits, axis=1)
    weight = jnp.sum(jnp.where(hits, gates[:, :, None], 0), axis=1).astype(jnp.float32) * SCALE
    rank = jnp.cumsum(member.astype(jnp.int32), axis=0) - 1
    slots = jnp.arange(capacity, dtype=jnp.int32)
    pick = jnp.logical_and(member[:, :, None], rank[:, :, None] == slots[None, None, :])
    select = jnp.where(pick, 1.0, 0.0).astype(jnp.float32)
    slot_gate = jnp.sum(select * weight[:, :, None], axis=0)
    return (select, slot_gate)


def expert_math(mine, w_own, w_other, hid):
    f32 = jnp.float32
    bf16 = jnp.bfloat16
    nt = (((1,), (1,)), ((), ()))
    n = mine.shape[0]
    flat = mine.reshape(-1, mine.shape[-1])
    pre_a = jnp.dot(flat, w_own, preferred_element_type=f32)
    pre_b = jnp.dot(flat, w_other, preferred_element_type=f32)
    pre = jnp.stack([pre_a, pre_b], axis=0).reshape(2, n, 2, -1, 3 * hid)
    gate_pre = pre[:, :, 0, :, :hid]
    up_pre = pre[:, :, 0, :, hid : 2 * hid]
    d_hidden = pre[:, :, 1, :, 2 * hid :]
    sig = jax.nn.sigmoid(gate_pre)
    act = gate_pre * sig
    hidden = (act * up_pre).astype(bf16)
    d_gate = (d_hidden * up_pre * sig * (1.0 + gate_pre * (1.0 - sig))).astype(bf16)
    d_up = (d_hidden * act).astype(bf16)
    zero = jnp.zeros_like(hidden)
    tok_side = jnp.concatenate([d_gate, d_up, zero], axis=-1)
    cot_side = jnp.concatenate([zero, zero, hidden], axis=-1)
    grad_side = jnp.stack([tok_side, cot_side], axis=2).reshape(2, -1, 3 * hid)
    out_side = jnp.stack([cot_side, tok_side], axis=2).reshape(2, -1, 3 * hid)
    results = lax.dot_general(out_side[0], w_own, nt, preferred_element_type=f32) + lax.dot_general(
        out_side[1], w_other, nt, preferred_element_type=f32
    )
    return results, grad_side[0], grad_side[1]


def per_device(tokens, out_cotangent, expert_ids, gate_fixed, w_gate, w_up, w_down):
    window = lax.axis_size("ex")
    zsize = lax.axis_size("ez")
    hid = w_gate.shape[2]
    f32 = jnp.float32
    swap = [(0, 1), (1, 0)]
    w_loc = jnp.concatenate([w_gate[0], w_up[0], w_down[0]], axis=1)
    w_all = lax.all_gather(w_loc, "dp", axis=0, tiled=False).reshape(-1, 3 * hid)
    w_other = lax.ppermute(w_all, "ec", swap)
    select, slot_gate = routing(expert_ids, gate_fixed, window, CAP)
    select_b = select.astype(jnp.bfloat16)
    slot_tokens = jnp.einsum("tec,tf->ecf", select_b, tokens, preferred_element_type=f32).astype(
        jnp.bfloat16
    )
    picked = jnp.einsum("tec,tf->ecf", select_b, out_cotangent, preferred_element_type=f32)
    slot_cot = (picked * slot_gate[:, :, None]).astype(jnp.bfloat16)
    payload = jnp.concatenate([slot_tokens, slot_cot], axis=1)
    width = payload.shape[-1]
    outgoing = jnp.broadcast_to(payload[:, None], (window, zsize, 2 * CAP, width)).reshape(
        window * zsize, 2 * CAP, width
    )
    mine = lax.all_to_all(outgoing, ("ex", "ez"), split_axis=0, concat_axis=0, tiled=True)
    partner = lax.ppermute(mine, "ec", swap)
    results, own_side, other_side = expert_math(mine, w_all, w_other, hid)
    got_side = lax.ppermute(other_side, "ec", swap)
    tn = (((0,), (0,)), ((), ()))
    chip_term = lax.dot_general(
        mine.reshape(-1, width), own_side, tn, preferred_element_type=f32
    ) + lax.dot_general(partner.reshape(-1, width), got_side, tn, preferred_element_type=f32)
    summed = lax.psum_scatter(
        chip_term.astype(jnp.bfloat16), "dp", scatter_dimension=0, tiled=True
    ).astype(f32)
    grad_gate = summed[:, :hid][None]
    grad_up = summed[:, hid : 2 * hid][None]
    grad_down = summed[:, 2 * hid :][None]
    pair = results.astype(jnp.bfloat16).reshape(window * zsize, 2 * CAP, width)
    returned = lax.all_to_all(pair, ("ex", "ez"), split_axis=0, concat_axis=0, tiled=True)
    combined = jnp.sum(
        returned.reshape(window, zsize, 2 * CAP, width).astype(f32), axis=1
    ).astype(jnp.bfloat16).reshape(window, 2, CAP, width)
    weighted = select * slot_gate[None, :, :]
    layer_out = jnp.einsum("tec,ecf->tf", weighted, combined[:, 0].astype(f32), precision=HIGH)
    token_grad = jnp.einsum("tec,ecf->tf", select_b, combined[:, 1], preferred_element_type=f32)
    return (
        layer_out.astype(jnp.bfloat16),
        token_grad.astype(jnp.bfloat16),
        grad_gate,
        grad_up,
        grad_down,
    )


def solution(mesh):
    n_dp = mesh.shape["dp"]
    n_exp = mesh.shape["expert"]
    devices = mesh.devices.reshape(n_dp, n_exp // SPLIT, SPLIT // 2, 2)
    grid = Mesh(devices, ("dp", "ex", "ez", "ec"))
    tok = P(("dp", "ex", "ez", "ec"), None)
    wsp = P(("ex", "ez", "ec"), "dp", None)
    return jax.shard_map(
        per_device,
        mesh=grid,
        in_specs=(tok, tok, tok, tok, wsp, wsp, wsp),
        out_specs=(tok, tok, wsp, wsp, wsp),
        check_vma=False,
    )
```

```python
import jax
import jax.numpy as jnp
from jax import lax
from jax.sharding import Mesh
from jax.sharding import PartitionSpec as P

SPLIT = 16
CAP = 4


SCALE = 2.0 ** (-16)
HIGH = lax.Precision.HIGHEST


def routing(ids, gates, window, capacity):
    wanted = jnp.arange(window, dtype=jnp.int32)
    hits = ids[:, :, None] == wanted[None, None, :]
    member = jnp.any(hits, axis=1)
    weight = jnp.sum(jnp.where(hits, gates[:, :, None], 0), axis=1).astype(jnp.float32) * SCALE
    rank = jnp.cumsum(member.astype(jnp.int32), axis=0) - 1
    slots = jnp.arange(capacity, dtype=jnp.int32)
    pick = jnp.logical_and(member[:, :, None], rank[:, :, None] == slots[None, None, :])
    select = jnp.where(pick, 1.0, 0.0).astype(jnp.float32)
    slot_gate = jnp.sum(select * weight[:, :, None], axis=0)
    return (select, slot_gate)


def expert_math(mine, w_two, hid):
    f32 = jnp.float32
    bf16 = jnp.bfloat16
    nt = (((1,), (1,)), ((), ()))
    tn = (((0,), (0,)), ((), ()))
    n = mine.shape[0]
    flat = mine.reshape(-1, mine.shape[-1])
    pre = jnp.dot(flat, w_two, preferred_element_type=f32).reshape(n, 2, -1, 2, 3 * hid)
    gate_pre = pre[:, 0, :, :, :hid]
    up_pre = pre[:, 0, :, :, hid : 2 * hid]
    d_hidden = pre[:, 1, :, :, 2 * hid :]
    sig = jax.nn.sigmoid(gate_pre)
    act = gate_pre * sig
    hidden = (act * up_pre).astype(bf16)
    d_gate = (d_hidden * up_pre * sig * (1.0 + gate_pre * (1.0 - sig))).astype(bf16)
    d_up = (d_hidden * act).astype(bf16)
    zero = jnp.zeros_like(hidden)
    tok_side = jnp.concatenate([d_gate, d_up, zero], axis=-1)
    cot_side = jnp.concatenate([zero, zero, hidden], axis=-1)
    grad_side = jnp.stack([tok_side, cot_side], axis=1).reshape(-1, 2 * 3 * hid)
    out_side = jnp.stack([cot_side, tok_side], axis=1).reshape(-1, 2 * 3 * hid)
    results = lax.dot_general(out_side, w_two, nt, preferred_element_type=f32)
    return results, grad_side.reshape(-1, 2, 3 * hid)


def per_device(tokens, out_cotangent, expert_ids, gate_fixed, w_gate, w_up, w_down):
    window = lax.axis_size("ex")
    zsize = lax.axis_size("ez")
    hid = w_gate.shape[2]
    f32 = jnp.float32
    swap = [(0, 1), (1, 0)]
    w_loc = jnp.concatenate([w_gate[0], w_up[0], w_down[0]], axis=1)
    w_all = lax.all_gather(w_loc, "dp", axis=0, tiled=False).reshape(-1, 3 * hid)
    w_other = lax.ppermute(w_all, "ec", swap)
    w_pair = jnp.stack([w_all, w_other], axis=1)
    w_two = w_pair.reshape(-1, 2 * 3 * hid)
    select, slot_gate = routing(expert_ids, gate_fixed, window, CAP)
    select_b = select.astype(jnp.bfloat16)
    slot_tokens = jnp.einsum("tec,tf->ecf", select_b, tokens, preferred_element_type=f32).astype(
        jnp.bfloat16
    )
    picked = jnp.einsum("tec,tf->ecf", select_b, out_cotangent, preferred_element_type=f32)
    slot_cot = (picked * slot_gate[:, :, None]).astype(jnp.bfloat16)
    payload = jnp.concatenate([slot_tokens, slot_cot], axis=1)
    width = payload.shape[-1]
    outgoing = jnp.broadcast_to(payload[:, None], (window, zsize, 2 * CAP, width)).reshape(
        window * zsize, 2 * CAP, width
    )
    mine = lax.all_to_all(outgoing, ("ex", "ez"), split_axis=0, concat_axis=0, tiled=True)
    partner = lax.ppermute(mine, "ec", swap)
    results, grad_side = expert_math(mine, w_two, hid)
    own_side = grad_side[:, 0]
    other_side = grad_side[:, 1]
    got_side = lax.ppermute(other_side, "ec", swap)
    tn = (((0,), (0,)), ((), ()))
    chip_term = lax.dot_general(
        mine.reshape(-1, width), own_side, tn, preferred_element_type=f32
    ) + lax.dot_general(partner.reshape(-1, width), got_side, tn, preferred_element_type=f32)
    summed = lax.psum_scatter(
        chip_term.astype(jnp.bfloat16), "dp", scatter_dimension=0, tiled=True
    ).astype(f32)
    grad_gate = summed[:, :hid][None]
    grad_up = summed[:, hid : 2 * hid][None]
    grad_down = summed[:, 2 * hid :][None]
    pair = results.astype(jnp.bfloat16).reshape(window * zsize, 2 * CAP, width)
    returned = lax.all_to_all(pair, ("ex", "ez"), split_axis=0, concat_axis=0, tiled=True)
    combined = jnp.sum(
        returned.reshape(window, zsize, 2 * CAP, width).astype(f32), axis=1
    ).astype(jnp.bfloat16).reshape(window, 2, CAP, width)
    weighted = select * slot_gate[None, :, :]
    layer_out = jnp.einsum("tec,ecf->tf", weighted, combined[:, 0].astype(f32), precision=HIGH)
    token_grad = jnp.einsum("tec,ecf->tf", select_b, combined[:, 1], preferred_element_type=f32)
    return (
        layer_out.astype(jnp.bfloat16),
        token_grad.astype(jnp.bfloat16),
        grad_gate,
        grad_up,
        grad_down,
    )


def solution(mesh):
    n_dp = mesh.shape["dp"]
    n_exp = mesh.shape["expert"]
    devices = mesh.devices.reshape(n_dp, n_exp // SPLIT, SPLIT // 2, 2)
    grid = Mesh(devices, ("dp", "ex", "ez", "ec"))
    tok = P(("dp", "ex", "ez", "ec"), None)
    wsp = P(("ex", "ez", "ec"), "dp", None)
    return jax.shard_map(
        per_device,
        mesh=grid,
        in_specs=(tok, tok, tok, tok, wsp, wsp, wsp),
        out_specs=(tok, tok, wsp, wsp, wsp),
        check_vma=False,
    )
```

```python
import jax
import jax.numpy as jnp
from jax import lax
from jax.sharding import Mesh
from jax.sharding import PartitionSpec as P

SPLIT = 16
CAP = 4


SCALE = 2.0 ** (-16)
HIGH = lax.Precision.HIGHEST


def routing(ids, gates, window, capacity):
    wanted = jnp.arange(window, dtype=jnp.int32)
    hits = ids[:, :, None] == wanted[None, None, :]
    member = jnp.any(hits, axis=1)
    weight = jnp.sum(jnp.where(hits, gates[:, :, None], 0), axis=1).astype(jnp.float32) * SCALE
    rank = jnp.cumsum(member.astype(jnp.int32), axis=0) - 1
    slots = jnp.arange(capacity, dtype=jnp.int32)
    pick = jnp.logical_and(member[:, :, None], rank[:, :, None] == slots[None, None, :])
    select = jnp.where(pick, 1.0, 0.0).astype(jnp.float32)
    slot_gate = jnp.sum(select * weight[:, :, None], axis=0)
    return (select, slot_gate)


def expert_math(mine, w_two, hid):
    f32 = jnp.float32
    bf16 = jnp.bfloat16
    nt = (((1,), (1,)), ((), ()))
    tn = (((0,), (0,)), ((), ()))
    n = mine.shape[0]
    flat = mine.reshape(-1, mine.shape[-1])
    pre = jnp.dot(flat, w_two, preferred_element_type=f32).reshape(n, 2, -1, 2, 3 * hid)
    gate_pre = pre[:, 0, :, :, :hid]
    up_pre = pre[:, 0, :, :, hid : 2 * hid]
    d_hidden = pre[:, 1, :, :, 2 * hid :]
    sig = jax.nn.sigmoid(gate_pre)
    act = gate_pre * sig
    hidden = (act * up_pre).astype(bf16)
    d_gate = (d_hidden * up_pre * sig * (1.0 + gate_pre * (1.0 - sig))).astype(bf16)
    d_up = (d_hidden * act).astype(bf16)
    zero = jnp.zeros_like(hidden)
    tok_side = jnp.concatenate([d_gate, d_up, zero], axis=-1)
    cot_side = jnp.concatenate([zero, zero, hidden], axis=-1)
    grad_side = jnp.stack([tok_side, cot_side], axis=1).reshape(-1, 2 * 3 * hid)
    out_side = jnp.stack([cot_side, tok_side], axis=1).reshape(-1, 2 * 3 * hid)
    results = lax.dot_general(out_side, w_two, nt, preferred_element_type=f32)
    return results, grad_side.reshape(-1, 2, 3 * hid)


def per_device(tokens, out_cotangent, expert_ids, gate_fixed, w_gate, w_up, w_down):
    window = lax.axis_size("ex")
    zsize = lax.axis_size("ez")
    hid = w_gate.shape[2]
    f32 = jnp.float32
    swap = [(0, 1), (1, 0)]
    w_loc = jnp.concatenate([w_gate[0], w_up[0], w_down[0]], axis=1)
    w_all = lax.all_gather(w_loc, "dp", axis=0, tiled=False).reshape(-1, 3 * hid)
    w_other = lax.ppermute(w_all, "ec", swap)
    w_pair = jnp.stack([w_all, w_other], axis=1)
    w_two = w_pair.reshape(-1, 2 * 3 * hid)
    select, slot_gate = routing(expert_ids, gate_fixed, window, CAP)
    select_b = select.astype(jnp.bfloat16)
    slot_tokens = jnp.einsum("tec,tf->ecf", select_b, tokens, preferred_element_type=f32).astype(
        jnp.bfloat16
    )
    picked = jnp.einsum("tec,tf->ecf", select_b, out_cotangent, preferred_element_type=f32)
    slot_cot = (picked * slot_gate[:, :, None]).astype(jnp.bfloat16)
    payload = jnp.concatenate([slot_tokens, slot_cot], axis=1)
    width = payload.shape[-1]
    outgoing = jnp.broadcast_to(payload[:, None], (window, zsize, 2 * CAP, width)).reshape(
        window * zsize, 2 * CAP, width
    )
    mine = lax.all_to_all(outgoing, ("ex", "ez"), split_axis=0, concat_axis=0, tiled=True)
    partner = lax.ppermute(mine, "ec", swap)
    results, grad_side = expert_math(mine, w_two, hid)
    own_side = grad_side[:, 0]
    other_side = grad_side[:, 1]
    got_side = lax.ppermute(other_side, "ec", swap)
    tn = (((0,), (0,)), ((), ()))
    chip_term = lax.dot_general(
        mine.reshape(-1, width), own_side, tn, preferred_element_type=f32
    ) + lax.dot_general(partner.reshape(-1, width), got_side, tn, preferred_element_type=f32)
    summed = lax.psum_scatter(
        chip_term.astype(jnp.bfloat16), "dp", scatter_dimension=0, tiled=True
    ).astype(f32)
    grad_gate = summed[:, :hid][None]
    grad_up = summed[:, hid : 2 * hid][None]
    grad_down = summed[:, 2 * hid :][None]
    pair = results.astype(jnp.bfloat16).reshape(window * zsize, 2 * CAP, width)
    returned = lax.all_to_all(pair, ("ex", "ez"), split_axis=0, concat_axis=0, tiled=True)
    combined = jnp.sum(
        returned.reshape(window, zsize, 2 * CAP, width).astype(f32), axis=1
    ).astype(jnp.bfloat16).reshape(window, 2, CAP, width)
    weighted = select * slot_gate[None, :, :]
    layer_out = jnp.einsum(
        "tec,ecf->tf", weighted, combined[:, 0].astype(f32), precision=lax.Precision.HIGH
    )
    token_grad = jnp.einsum("tec,ecf->tf", select_b, combined[:, 1], preferred_element_type=f32)
    return (
        layer_out.astype(jnp.bfloat16),
        token_grad.astype(jnp.bfloat16),
        grad_gate,
        grad_up,
        grad_down,
    )


def solution(mesh):
    n_dp = mesh.shape["dp"]
    n_exp = mesh.shape["expert"]
    devices = mesh.devices.reshape(n_dp, n_exp // SPLIT, SPLIT // 2, 2)
    grid = Mesh(devices, ("dp", "ex", "ez", "ec"))
    tok = P(("dp", "ex", "ez", "ec"), None)
    wsp = P(("ex", "ez", "ec"), "dp", None)
    return jax.shard_map(
        per_device,
        mesh=grid,
        in_specs=(tok, tok, tok, tok, wsp, wsp, wsp),
        out_specs=(tok, tok, wsp, wsp, wsp),
        check_vma=False,
    )
```
